512 devices in a mesh: row: 16 (over y_lo, z), col: 32 (over x, y_hi, core).
Axes of the slice: x: 4, y: 8 (y_hi: 4, y_lo: 2; y = y_hi * 2 + y_lo), z: 8, core: 2. Of those that a mesh axis runs over, the one named last changes fastest.
Arguments:
- hidden: bfloat16 [4096, 2048], P('col', 'row'), may hold values from -6 to 6
- qkv_weight: bfloat16 [2048, 3, 2048], P('col', None, 'row'), may hold values from -0.125 to 0.125
- q_gain: float32 [2048], P('row'), may hold values from 0.1 to 1.9
- k_gain: float32 [2048], P('row'), may hold values from 0.1 to 1.9
- key_cache: bfloat16 [512, 128, 2048], P('col', None, 'row'), may hold values from -120 to 120
- value_cache: bfloat16 [512, 128, 2048], P('col', None, 'row'), may hold values from -6 to 6
- page_table: int32 [512], replicated, may hold values from 0 to 511, each once
- suffix_lengths: int32 [4], replicated, may hold values from 1 to 2048, 4096 in all
- token_slot: int32 [4096], replicated, may hold values from 0 to 4095, each once
- o_weight: bfloat16 [2048, 2048], P('row', 'col'), may hold values from -0.125 to 0.125
- norm_gain: float32 [2048], P('row'), may hold values from 0.1 to 1.9
Outputs:
- layer_out: float32 [4096, 2048], P('col', 'row')
The draws below stay inside these ranges and needn't reach their ends.
Inputs may be any that keep to these rules, and one draw needn't show every extreme that they name: `page_table`: every cache slot holds exactly one page; slot s lies with index s // 16 of col. `suffix_lengths`: they sum to 4096; the largest is exactly 2048. `token_slot`: each packed position occurs in exactly one row; packed positions run group after group.
All inputs are finite; a program needn't handle non-finite values.
Results may differ from the reference program's by a relative error of at most 0.012.
Values may be sent and summed in bfloat16 or wider, within the bound.
No kernel may reach another device: no remote copies, remote signals or barrier semaphores. Data moves between devices by JAX's collectives and lax.ppermute only.
A program may use at most 64 MiB of HBM per device.

```python
import math
import jax
import jax.numpy as jnp
import numpy as np
from jax import lax

D = 2048
HD = 128
PAGE = 128
GROUPS = 4
TOKENS = 4096
PAGES = 512
PREFIX = 16384


def draw_key_cache(key, part):
    first = jax.random.fold_in(key, 0)
    base = jax.random.truncated_normal(first, -4.0, 4.0, (PAGES, PAGE, D), jnp.float32)
    return base.astype(jnp.bfloat16)


def steps_of(stream_key, extent, cuts, low, largest):
    level, own = 1.0, jax.random.fold_in(stream_key, 6)
    for dim, parts in cuts:
        steps = jnp.exp(jax.random.uniform(jax.random.fold_in(own, dim), (parts,), jnp.float32, low / len(cuts), largest / len(cuts)))
        level = level * jnp.repeat(steps, extent[dim] // parts).reshape([-1 if axis == dim else 1 for axis in range(len(extent))])
    return level


def length_profile(count, total, limit, skew):
    weights = [(1 << 20) // math.isqrt(grade ** skew) + 1 for grade in range(2, count + 1)]
    rest, holding = total - limit - (count - 1), [1] * (count - 1)
    while rest > 0:
        free = [i for i in range(count - 1) if holding[i] < limit]
        mass, left = sum([weights[i] for i in free]), rest
        for i in free:
            more = min(limit - holding[i], max(1, left * weights[i] // mass), rest)
            holding[i] = holding[i] + more
            rest = rest - more
    return np.array([limit] + holding)


def uneven(own_key, amount, total, most, slope):
    if amount == 2:
        one = jax.random.randint(own_key, (), max(1, total - most), min(most, total - 1) + 1)
        return jnp.stack([one, total - one])
    lengths = jnp.asarray(length_profile(amount, total, most, slope), jnp.int32)
    couples = (amount - 1) // 2
    source_of, taker = lengths[1:1 + 2 * couples:2], lengths[2:2 + 2 * couples:2]
    room = jnp.minimum(source_of - 1, most - taker)
    passed = jax.random.randint(jax.random.fold_in(own_key, 1), (couples,), 0, 1 << 20) % (room + 1)
    lengths = lengths.at[1:1 + 2 * couples:2].set(source_of - passed).at[2:2 + 2 * couples:2].set(taker + passed)
    return lengths[jax.random.permutation(jax.random.fold_in(own_key, 2), amount)]


def scatter_about(rng, shape, scale, limit, cuts=(), held_as=jnp.bfloat16):
    level = steps_of(rng, shape, cuts, -0.22, 0.18) if cuts else 1.0
    values = jax.random.normal(rng, shape, jnp.float32) * scale * level
    return jnp.minimum(jnp.maximum(values, -limit), limit).astype(held_as)


def setup_inputs(seed: int = 0) -> dict:
    seeds = jax.random.split(jax.random.key(seed), 12)
    return {
        "hidden": scatter_about(seeds[0], (TOKENS, D), 1.0, 6.0, ((0, 32), (1, 16))),
        "qkv_weight": scatter_about(seeds[1], (D, 3, D), D ** -0.5, 0.125, ((0, 32), (2, 16))),
        "q_gain": jnp.clip(1.0 + 0.18 * jax.random.normal(seeds[2], (D,), jnp.float32), 0.1, 1.9),
        "k_gain": jnp.clip(1.0 + 0.18 * jax.random.normal(seeds[3], (D,), jnp.float32), 0.1, 1.9),
        "key_cache": draw_key_cache(jax.random.fold_in(seeds[11], 71), 0),
        "value_cache": scatter_about(seeds[5], (PAGES, PAGE, D), 1.0, 6.0, ((0, 32), (2, 16))),
        "page_table": jax.random.permutation(seeds[6], PAGES).astype(jnp.int32),
        "suffix_lengths": uneven(seeds[7], GROUPS, TOKENS, TOKENS // 2, 2).astype(jnp.int32),
        "token_slot": jax.random.permutation(seeds[8], TOKENS).astype(jnp.int32),
        "o_weight": scatter_about(seeds[9], (D, D), D ** -0.5, 0.125, ((0, 16), (1, 32))),
        "norm_gain": jnp.clip(1.0 + 0.18 * jax.random.normal(seeds[10], (D,), jnp.float32), 0.1, 1.9),
    }


EPS = 1e-06
THETA = 500000.0
NEG = -1e+30

def rotate(states, position):
    half = states.shape[-1] // 2
    freq = THETA ** (-(jnp.arange(half, dtype=jnp.float32) * 2.0 / states.shape[-1]))
    angle = position.astype(jnp.float32)[:, None] * freq[None, :]
    cosine = jnp.cos(angle)[:, None, :]
    sine = jnp.sin(angle)[:, None, :]
    first = states[..., :half]
    second = states[..., half:]
    return jnp.concatenate([first * cosine - second * sine, second * cosine + first * sine], axis=-1)

def group_of(slots, ends):
    return lax.optimization_barrier(jnp.sum((ends[None, :] <= slots[:, None]).astype(jnp.int32), axis=1))

def partial_softmax(scores, values, allowed):
    scores = jnp.where(allowed, scores, NEG)
    highest = lax.optimization_barrier(jnp.max(scores, axis=-1))
    weights = jnp.exp(scores - highest[..., None])
    summed = lax.optimization_barrier(jnp.sum(weights, axis=-1))
    rounded = lax.optimization_barrier(weights.astype(jnp.bfloat16))
    numer = jnp.einsum('qhk,khd->qhd', rounded.astype(jnp.float32), values.astype(jnp.float32))
    return (highest, summed, numer)

def merge_parts(pieces):
    biggest = pieces[0][0]
    for entry in pieces[1:]:
        biggest = jnp.maximum(biggest, entry[0])
    denom = jnp.zeros_like(biggest)
    numer = jnp.zeros_like(pieces[0][2])
    for entry in pieces:
        factor = jnp.exp(entry[0] - biggest)
        denom = denom + entry[1] * factor
        numer = numer + entry[2] * factor[..., None]
    return numer / denom[..., None]

def reference(hidden, qkv_weight, q_gain, k_gain, key_cache, value_cache, page_table, suffix_lengths, token_slot, o_weight, norm_gain):
    heads = D // HD
    count_all = hidden.shape[0]
    projected = jnp.einsum('td,dcf->tcf', hidden.astype(jnp.float32), qkv_weight.astype(jnp.float32))

    def qk_norm(raw, gain):
        return raw * lax.rsqrt(lax.optimization_barrier(jnp.mean(raw * raw, axis=-1, keepdims=True)) + EPS) * gain.astype(jnp.float32)
    ends = jnp.cumsum(suffix_lengths).astype(jnp.int32)
    starts = (ends - suffix_lengths).astype(jnp.int32)
    groups = group_of(token_slot, ends)
    onehot = groups[:, None] == jnp.arange(GROUPS, dtype=jnp.int32)[None, :]
    begin = lax.optimization_barrier(jnp.sum(jnp.where(onehot, starts[None, :], 0), axis=1)).astype(jnp.int32)
    position = PREFIX + token_slot - begin
    query_rot = rotate(qk_norm(projected[:, 0], q_gain).reshape(count_all, heads, HD), position).astype(jnp.bfloat16)
    key_rot = rotate(qk_norm(projected[:, 1], k_gain).reshape(count_all, heads, HD), position).astype(jnp.bfloat16)
    value_rows = projected[:, 2].astype(jnp.bfloat16).reshape(count_all, heads, HD)
    order = jnp.argsort(token_slot).astype(jnp.int32)
    packed_query = query_rot[order]
    packed_key = key_rot[order]
    packed_value = value_rows[order]
    packed_slot = jnp.arange(count_all, dtype=jnp.int32)
    packed_group = group_of(packed_slot, ends)
    page_keys = key_cache[page_table].reshape(GROUPS, PREFIX, heads, HD)
    page_values = value_cache[page_table].reshape(GROUPS, PREFIX, heads, HD)
    block = min(128, count_all)
    scale = 1.0 / math.sqrt(HD)

    def one_block(number):
        first = (number * block).astype(jnp.int32)
        query_blk = lax.dynamic_slice_in_dim(packed_query, first, block).astype(jnp.float32)
        group_blk = lax.dynamic_slice_in_dim(packed_group, first, block)
        slot_blk = first + jnp.arange(block, dtype=jnp.int32)
        scores = jnp.einsum('qhd,khd->qhk', query_blk, packed_key.astype(jnp.float32)) * scale
        allowed = (packed_group[None, :] == group_blk[:, None]) & (packed_slot[None, :] <= slot_blk[:, None])
        pieces = [partial_softmax(scores, packed_value, allowed[:, None, :])]
        for member in range(GROUPS):
            inside = group_blk == member

            def compute(unused, member=member, inside=inside):
                prefix_scores = jnp.einsum('qhd,khd->qhk', query_blk, page_keys[member].astype(jnp.float32)) * scale
                highest, summed, numer = partial_softmax(prefix_scores, page_values[member], jnp.ones(prefix_scores.shape, dtype=bool))
                return (jnp.where(inside[:, None], highest, NEG), jnp.where(inside[:, None], summed, 0.0), jnp.where(inside[:, None, None], numer, 0.0))

            def skip(unused):
                return (jnp.full((block, heads), NEG, jnp.float32), jnp.zeros((block, heads), jnp.float32), jnp.zeros((block, heads, HD), jnp.float32))
            pieces.append(lax.cond(jnp.any(inside), compute, skip, 0))
        return merge_parts(pieces)
    attn_packed = lax.map(one_block, jnp.arange(count_all // block, dtype=jnp.int32))
    attention = attn_packed.reshape(count_all, D)[token_slot].astype(jnp.bfloat16)
    mixed = jnp.dot(attention, o_weight, preferred_element_type=jnp.float32)
    result = hidden.astype(jnp.float32) + mixed * lax.rsqrt(lax.optimization_barrier(jnp.mean(mixed * mixed, axis=-1, keepdims=True)) + EPS) * norm_gain.astype(jnp.float32)
    return result
```

```python
import math

import jax
import jax.numpy as jnp
from jax import lax
from jax.sharding import PartitionSpec as P

D = 2048
HD = 128


EPS = 1e-06
THETA = 500000.0
NEG = -1e30


def rotate(states, position):
    half = states.shape[-1] // 2
    freq = THETA ** (-(jnp.arange(half, dtype=jnp.float32) * 2.0 / states.shape[-1]))
    angle = position.astype(jnp.float32)[:, None] * freq[None, :]
    cosine = jnp.cos(angle)
    sine = jnp.sin(angle)
    first = states[..., :half]
    second = states[..., half:]
    return jnp.concatenate(
        [first * cosine - second * sine, second * cosine + first * sine], axis=-1
    )


def group_of(slots, ends):
    return jnp.sum((ends[None, :] <= slots[:, None]).astype(jnp.int32), axis=1)


def masked_partial(scores, allowed, values):
    scores = jnp.where(allowed, scores, NEG)
    top = jnp.max(scores, axis=-1)
    weights = jnp.where(allowed, jnp.exp(scores - top[:, None]), 0.0)
    total = jnp.sum(weights, axis=-1)
    numer = jnp.dot(weights.astype(jnp.bfloat16), values, preferred_element_type=jnp.float32)
    return top, total, numer


def per_device(
    hidden,
    qkv_weight,
    q_gain,
    k_gain,
    key_cache,
    value_cache,
    page_table,
    suffix_lengths,
    token_slot,
    o_weight,
    norm_gain,
):
    tok_here = hidden.shape[0]
    local_width = q_gain.shape[0]
    group_count = suffix_lengths.shape[0]
    page_size = key_cache.shape[1]
    slots_here = key_cache.shape[0]
    page_total = page_table.shape[0]
    prefix_len = page_total * page_size // group_count
    scale = 1.0 / math.sqrt(HD)
    column = lax.axis_index("col")

    hidden_t = lax.all_gather(hidden.T, "row", axis=0, tiled=True)
    weight_all = lax.all_gather(qkv_weight, "col", axis=0, tiled=True)
    out_weight_t = lax.all_gather(o_weight.T, "col", axis=0, tiled=True)

    projected = jnp.einsum(
        "dt,dcf->tcf", hidden_t, weight_all, preferred_element_type=jnp.float32
    )
    query_raw = projected[:, 0]
    key_raw = projected[:, 1]
    value_raw = projected[:, 2]
    squares = lax.psum(
        jnp.stack([jnp.sum(query_raw * query_raw, axis=1), jnp.sum(key_raw * key_raw, axis=1)]),
        "row",
    )
    query_norm = query_raw * lax.rsqrt(squares[0] / D + EPS)[:, None] * q_gain
    key_norm = key_raw * lax.rsqrt(squares[1] / D + EPS)[:, None] * k_gain
    ends = jnp.cumsum(suffix_lengths)
    starts = ends - suffix_lengths
    my_slot = lax.dynamic_slice_in_dim(token_slot, column * tok_here, tok_here)
    my_group = group_of(my_slot, ends)
    begin = jnp.sum(
        jnp.where(
            my_group[:, None] == jnp.arange(group_count, dtype=jnp.int32)[None, :],
            starts[None, :],
            0,
        ),
        axis=1,
    )
    position = prefix_len + my_slot - begin
    query_rot = rotate(query_norm, position).astype(jnp.bfloat16)
    key_rot = rotate(key_norm, position).astype(jnp.bfloat16)
    value_here = value_raw.astype(jnp.bfloat16)

    packed = jnp.concatenate([query_rot, key_rot, value_here], axis=1)
    gathered = lax.all_gather(packed, "col", axis=0, tiled=True)
    count_all = gathered.shape[0]
    cols = count_all // tok_here
    all_query = gathered[:, :local_width]
    all_key = gathered[:, local_width : 2 * local_width]
    all_value = gathered[:, 2 * local_width :]

    their_group = group_of(token_slot, ends)
    allowed = (their_group[None, :] == my_group[:, None]) & (
        token_slot[None, :] <= my_slot[:, None]
    )
    suffix_scores = (
        jnp.dot(query_rot, all_key.T, preferred_element_type=jnp.float32) * scale
    )
    suffix_top, suffix_sum, suffix_acc = masked_partial(suffix_scores, allowed, all_value)

    page_slots = column * slots_here + jnp.arange(slots_here, dtype=jnp.int32)
    page_index = jnp.sum(
        jnp.where(
            page_table[None, :] == page_slots[:, None],
            jnp.arange(page_total, dtype=jnp.int32)[None, :],
            0,
        ),
        axis=1,
    )
    slot_group = page_index // (page_total // group_count)
    key_group = jnp.repeat(slot_group, page_size)
    page_keys = key_cache.reshape(slots_here * page_size, local_width)
    page_values = value_cache.reshape(slots_here * page_size, local_width)

    block = 512
    blocks = count_all // block

    def one_block(inputs):
        queries, groups = inputs
        scores = jnp.dot(queries, page_keys.T, preferred_element_type=jnp.float32) * scale
        return masked_partial(scores, groups[:, None] == key_group[None, :], page_values)

    tops, sums, numers = lax.map(
        one_block,
        (all_query.reshape(blocks, block, local_width), their_group.reshape(blocks, block)),
    )
    numers = numers.reshape(cols, tok_here, local_width)
    tops = tops.reshape(cols, 1, tok_here)
    sums = sums.reshape(cols, 1, tok_here)
    outgoing = jnp.concatenate([numers, tops, sums], axis=1)
    incoming = lax.all_to_all(outgoing, "col", split_axis=0, concat_axis=0, tiled=True)
    got_acc = incoming[:, :tok_here, :]
    got_top = incoming[:, tok_here, :]
    got_sum = incoming[:, tok_here + 1, :]

    biggest = jnp.maximum(suffix_top, jnp.max(got_top, axis=0))
    weight_self = jnp.exp(suffix_top - biggest)
    weight_owner = jnp.exp(got_top - biggest[None])
    denominator = suffix_sum * weight_self + jnp.sum(got_sum * weight_owner, axis=0)
    numerator = suffix_acc * weight_self[:, None] + jnp.sum(
        got_acc * weight_owner[..., None], axis=0
    )
    attention = (numerator / denominator[:, None]).astype(jnp.bfloat16)
    mixed = jnp.einsum(
        "th,oh->to", attention, out_weight_t, preferred_element_type=jnp.float32
    )
    branch = lax.psum_scatter(mixed, "row", scatter_dimension=1, tiled=True)
    mean_sq = lax.psum(jnp.sum(branch * branch, axis=1), "row") / D
    result = hidden.astype(jnp.float32) + branch * lax.rsqrt(mean_sq + EPS)[:, None] * norm_gain
    return result


def solution(mesh):
    return jax.shard_map(
        per_device,
        mesh=mesh,
        in_specs=(
            P("col", "row"),
            P("col", None, "row"),
            P("row"),
            P("row"),
            P("col", None, "row"),
            P("col", None, "row"),
            P(),
            P(),
            P(),
            P("row", "col"),
            P("row"),
        ),
        out_specs=P("col", "row"),
        check_vma=False,
    )
```

```python
import math

import jax
import jax.numpy as jnp
from jax import lax
from jax.sharding import PartitionSpec as P

D = 2048
HD = 128


EPS = 1e-06
THETA = 500000.0
NEG = -1e30


def rotate(states, position):
    half = states.shape[-1] // 2
    freq = THETA ** (-(jnp.arange(half, dtype=jnp.float32) * 2.0 / states.shape[-1]))
    angle = position.astype(jnp.float32)[:, None] * freq[None, :]
    cosine = jnp.cos(angle)
    sine = jnp.sin(angle)
    first = states[..., :half]
    second = states[..., half:]
    return jnp.concatenate(
        [first * cosine - second * sine, second * cosine + first * sine], axis=-1
    )


def group_of(slots, ends):
    return jnp.sum((ends[None, :] <= slots[:, None]).astype(jnp.int32), axis=1)


def masked_partial(scores, allowed, values):
    scores = jnp.where(allowed, scores, NEG)
    top = jnp.max(scores, axis=-1)
    weights = jnp.where(allowed, jnp.exp(scores - top[:, None]), 0.0)
    total = jnp.sum(weights, axis=-1)
    numer = jnp.dot(weights.astype(jnp.bfloat16), values, preferred_element_type=jnp.float32)
    return top, total, numer


def per_device(
    hidden,
    qkv_weight,
    q_gain,
    k_gain,
    key_cache,
    value_cache,
    page_table,
    suffix_lengths,
    token_slot,
    o_weight,
    norm_gain,
):
    tok_here = hidden.shape[0]
    local_width = q_gain.shape[0]
    group_count = suffix_lengths.shape[0]
    page_size = key_cache.shape[1]
    slots_here = key_cache.shape[0]
    page_total = page_table.shape[0]
    prefix_len = page_total * page_size // group_count
    scale = 1.0 / math.sqrt(HD)
    column = lax.axis_index("col")

    hidden_t = lax.all_gather(hidden.T, "row", axis=0, tiled=True)
    weights_here = jnp.concatenate([qkv_weight, o_weight.T[:, None, :]], axis=1)
    weights_all = lax.all_gather(weights_here, "col", axis=0, tiled=True)
    weight_all = weights_all[:, :3]
    out_weight_t = weights_all[:, 3]

    projected = jnp.einsum(
        "dt,dcf->tcf", hidden_t, weight_all, preferred_element_type=jnp.float32
    )
    query_raw = projected[:, 0]
    key_raw = projected[:, 1]
    value_raw = projected[:, 2]
    squares = lax.psum(
        jnp.stack([jnp.sum(query_raw * query_raw, axis=1), jnp.sum(key_raw * key_raw, axis=1)]),
        "row",
    )
    query_norm = query_raw * lax.rsqrt(squares[0] / D + EPS)[:, None] * q_gain
    key_norm = key_raw * lax.rsqrt(squares[1] / D + EPS)[:, None] * k_gain
    ends = jnp.cumsum(suffix_lengths)
    starts = ends - suffix_lengths
    my_slot = lax.dynamic_slice_in_dim(token_slot, column * tok_here, tok_here)
    my_group = group_of(my_slot, ends)
    begin = jnp.sum(
        jnp.where(
            my_group[:, None] == jnp.arange(group_count, dtype=jnp.int32)[None, :],
            starts[None, :],
            0,
        ),
        axis=1,
    )
    position = prefix_len + my_slot - begin
    query_rot = rotate(query_norm, position).astype(jnp.bfloat16)
    key_rot = rotate(key_norm, position).astype(jnp.bfloat16)
    value_here = value_raw.astype(jnp.bfloat16)

    packed = jnp.concatenate([query_rot, key_rot, value_here], axis=1)
    gathered = lax.all_gather(packed, "col", axis=0, tiled=True)
    count_all = gathered.shape[0]
    cols = count_all // tok_here
    all_query = gathered[:, :local_width]
    all_key = gathered[:, local_width : 2 * local_width]
    all_value = gathered[:, 2 * local_width :]

    their_group = group_of(token_slot, ends)
    allowed = (their_group[None, :] == my_group[:, None]) & (
        token_slot[None, :] <= my_slot[:, None]
    )
    suffix_scores = (
        jnp.dot(query_rot, all_key.T, preferred_element_type=jnp.float32) * scale
    )
    suffix_top, suffix_sum, suffix_acc = masked_partial(suffix_scores, allowed, all_value)

    page_slots = column * slots_here + jnp.arange(slots_here, dtype=jnp.int32)
    page_index = jnp.sum(
        jnp.where(
            page_table[None, :] == page_slots[:, None],
            jnp.arange(page_total, dtype=jnp.int32)[None, :],
            0,
        ),
        axis=1,
    )
    slot_group = page_index // (page_total // group_count)
    key_group = jnp.repeat(slot_group, page_size)
    page_keys = key_cache.reshape(slots_here * page_size, local_width)
    page_values = value_cache.reshape(slots_here * page_size, local_width)

    block = 512
    blocks = count_all // block

    def one_block(inputs):
        queries, groups = inputs
        scores = jnp.dot(queries, page_keys.T, preferred_element_type=jnp.float32) * scale
        return masked_partial(scores, groups[:, None] == key_group[None, :], page_values)

    tops, sums, numers = lax.map(
        one_block,
        (all_query.reshape(blocks, block, local_width), their_group.reshape(blocks, block)),
    )
    numers = numers.reshape(cols, tok_here, local_width)
    tops = tops.reshape(cols, 1, tok_here)
    sums = sums.reshape(cols, 1, tok_here)
    outgoing = jnp.concatenate([numers, tops, sums], axis=1)
    incoming = lax.all_to_all(outgoing, "col", split_axis=0, concat_axis=0, tiled=True)
    got_acc = incoming[:, :tok_here, :]
    got_top = incoming[:, tok_here, :]
    got_sum = incoming[:, tok_here + 1, :]

    biggest = jnp.maximum(suffix_top, jnp.max(got_top, axis=0))
    weight_self = jnp.exp(suffix_top - biggest)
    weight_owner = jnp.exp(got_top - biggest[None])
    denominator = suffix_sum * weight_self + jnp.sum(got_sum * weight_owner, axis=0)
    numerator = suffix_acc * weight_self[:, None] + jnp.sum(
        got_acc * weight_owner[..., None], axis=0
    )
    attention = (numerator / denominator[:, None]).astype(jnp.bfloat16)
    mixed = jnp.einsum(
        "th,oh->to", attention, out_weight_t, preferred_element_type=jnp.float32
    )
    branch = lax.psum_scatter(mixed, "row", scatter_dimension=1, tiled=True)
    mean_sq = lax.psum(jnp.sum(branch * branch, axis=1), "row") / D
    result = hidden.astype(jnp.float32) + branch * lax.rsqrt(mean_sq + EPS)[:, None] * norm_gain
    return result


def solution(mesh):
    return jax.shard_map(
        per_device,
        mesh=mesh,
        in_specs=(
            P("col", "row"),
            P("col", None, "row"),
            P("row"),
            P("row"),
            P("col", None, "row"),
            P("col", None, "row"),
            P(),
            P(),
            P(),
            P("row", "col"),
            P("row"),
        ),
        out_specs=P("col", "row"),
        check_vma=False,
    )
```

```python
import math

import jax
import jax.numpy as jnp
from jax import lax
from jax.sharding import PartitionSpec as P

D = 2048
HD = 128


EPS = 1e-06
THETA = 500000.0
NEG = -1e30


def rotate(states, position):
    half = states.shape[-1] // 2
    freq = THETA ** (-(jnp.arange(half, dtype=jnp.float32) * 2.0 / states.shape[-1]))
    angle = position.astype(jnp.float32)[:, None] * freq[None, :]
    cosine = jnp.cos(angle)
    sine = jnp.sin(angle)
    first = states[..., :half]
    second = states[..., half:]
    return jnp.concatenate(
        [first * cosine - second * sine, second * cosine + first * sine], axis=-1
    )


def group_of(slots, ends):
    return jnp.sum((ends[None, :] <= slots[:, None]).astype(jnp.int32), axis=1)


def masked_partial(scores, allowed, values):
    scores = jnp.where(allowed, scores, NEG)
    top = jnp.max(scores, axis=-1)
    weights = jnp.where(allowed, jnp.exp(scores - top[:, None]), 0.0)
    total = jnp.sum(weights, axis=-1)
    numer = jnp.dot(weights.astype(jnp.bfloat16), values, preferred_element_type=jnp.float32)
    return top, total, numer


def butterfly_sum(x, axis, n):
    step = 1
    while step < n:
        x = x + lax.ppermute(x, axis, [(i, i ^ step) for i in range(n)])
        step *= 2
    return x


def halving_scatter(x, axis, n):
    rows = x.shape[0]
    me = lax.axis_index(axis)
    buf = x.reshape(rows, n, x.shape[1] // n)
    step = n // 2
    while step >= 1:
        half = buf.shape[1] // 2
        upper = (me // step) % 2
        keep = lax.dynamic_slice_in_dim(buf, upper * half, half, axis=1)
        send = lax.dynamic_slice_in_dim(buf, (1 - upper) * half, half, axis=1)
        buf = keep + lax.ppermute(send, axis, [(i, i ^ step) for i in range(n)])
        step //= 2
    return buf.reshape(rows, -1)


def doubling_gather(x, axis, n):
    me = lax.axis_index(axis)
    buf = x
    step = 1
    while step < n:
        other = lax.ppermute(buf, axis, [(i, i ^ step) for i in range(n)])
        upper = (me // step) % 2
        lo = jnp.where(upper == 0, buf, other)
        hi = jnp.where(upper == 0, other, buf)
        buf = jnp.concatenate([lo, hi], axis=0)
        step *= 2
    return buf


def per_device(
    hidden,
    qkv_weight,
    q_gain,
    k_gain,
    key_cache,
    value_cache,
    page_table,
    suffix_lengths,
    token_slot,
    o_weight,
    norm_gain,
):
    tok_here = hidden.shape[0]
    local_width = q_gain.shape[0]
    group_count = suffix_lengths.shape[0]
    page_size = key_cache.shape[1]
    slots_here = key_cache.shape[0]
    page_total = page_table.shape[0]
    prefix_len = page_total * page_size // group_count
    scale = 1.0 / math.sqrt(HD)
    column = lax.axis_index("col")

    rows_n = D // local_width
    hidden_t = doubling_gather(hidden.T, "row", rows_n)
    weights_here = jnp.concatenate([qkv_weight, o_weight.T[:, None, :]], axis=1)
    weights_all = lax.all_gather(weights_here, "col", axis=0, tiled=True)
    weight_all = weights_all[:, :3]
    out_weight_t = weights_all[:, 3]

    projected = jnp.einsum(
        "dt,dcf->tcf", hidden_t, weight_all, preferred_element_type=jnp.float32
    )
    query_raw = projected[:, 0]
    key_raw = projected[:, 1]
    value_raw = projected[:, 2]
    squares = butterfly_sum(
        jnp.stack([jnp.sum(query_raw * query_raw, axis=1), jnp.sum(key_raw * key_raw, axis=1)]),
        "row",
        rows_n,
    )
    query_norm = query_raw * lax.rsqrt(squares[0] / D + EPS)[:, None] * q_gain
    key_norm = key_raw * lax.rsqrt(squares[1] / D + EPS)[:, None] * k_gain
    ends = jnp.cumsum(suffix_lengths)
    starts = ends - suffix_lengths
    my_slot = lax.dynamic_slice_in_dim(token_slot, column * tok_here, tok_here)
    my_group = group_of(my_slot, ends)
    begin = jnp.sum(
        jnp.where(
            my_group[:, None] == jnp.arange(group_count, dtype=jnp.int32)[None, :],
            starts[None, :],
            0,
        ),
        axis=1,
    )
    position = prefix_len + my_slot - begin
    query_rot = rotate(query_norm, position).astype(jnp.bfloat16)
    key_rot = rotate(key_norm, position).astype(jnp.bfloat16)
    value_here = value_raw.astype(jnp.bfloat16)

    packed = jnp.concatenate([query_rot, key_rot, value_here], axis=1)
    gathered = lax.all_gather(packed, "col", axis=0, tiled=True)
    count_all = gathered.shape[0]
    cols = count_all // tok_here
    all_query = gathered[:, :local_width]
    all_key = gathered[:, local_width : 2 * local_width]
    all_value = gathered[:, 2 * local_width :]

    their_group = group_of(token_slot, ends)
    allowed = (their_group[None, :] == my_group[:, None]) & (
        token_slot[None, :] <= my_slot[:, None]
    )
    suffix_scores = (
        jnp.dot(query_rot, all_key.T, preferred_element_type=jnp.float32) * scale
    )
    suffix_top, suffix_sum, suffix_acc = masked_partial(suffix_scores, allowed, all_value)

    page_slots = column * slots_here + jnp.arange(slots_here, dtype=jnp.int32)
    page_index = jnp.sum(
        jnp.where(
            page_table[None, :] == page_slots[:, None],
            jnp.arange(page_total, dtype=jnp.int32)[None, :],
            0,
        ),
        axis=1,
    )
    slot_group = page_index // (page_total // group_count)
    key_group = jnp.repeat(slot_group, page_size)
    page_keys = key_cache.reshape(slots_here * page_size, local_width)
    page_values = value_cache.reshape(slots_here * page_size, local_width)

    block = 512
    blocks = count_all // block

    def one_block(inputs):
        queries, groups = inputs
        scores = jnp.dot(queries, page_keys.T, preferred_element_type=jnp.float32) * scale
        return masked_partial(scores, groups[:, None] == key_group[None, :], page_values)

    tops, sums, numers = lax.map(
        one_block,
        (all_query.reshape(blocks, block, local_width), their_group.reshape(blocks, block)),
    )
    numers = numers.reshape(cols, tok_here, local_width)
    tops = tops.reshape(cols, 1, tok_here)
    sums = sums.reshape(cols, 1, tok_here)
    outgoing = jnp.concatenate([numers, tops, sums], axis=1)
    incoming = lax.all_to_all(outgoing, "col", split_axis=0, concat_axis=0, tiled=True)
    got_acc = incoming[:, :tok_here, :]
    got_top = incoming[:, tok_here, :]
    got_sum = incoming[:, tok_here + 1, :]

    biggest = jnp.maximum(suffix_top, jnp.max(got_top, axis=0))
    weight_self = jnp.exp(suffix_top - biggest)
    weight_owner = jnp.exp(got_top - biggest[None])
    denominator = suffix_sum * weight_self + jnp.sum(got_sum * weight_owner, axis=0)
    numerator = suffix_acc * weight_self[:, None] + jnp.sum(
        got_acc * weight_owner[..., None], axis=0
    )
    attention = (numerator / denominator[:, None]).astype(jnp.bfloat16)
    mixed = jnp.einsum(
        "th,oh->to", attention, out_weight_t, preferred_element_type=jnp.float32
    )
    branch = halving_scatter(mixed, "row", rows_n)
    mean_sq = butterfly_sum(jnp.sum(branch * branch, axis=1), "row", rows_n) / D
    result = hidden.astype(jnp.float32) + branch * lax.rsqrt(mean_sq + EPS)[:, None] * norm_gain
    return result


def solution(mesh):
    return jax.shard_map(
        per_device,
        mesh=mesh,
        in_specs=(
            P("col", "row"),
            P("col", None, "row"),
            P("row"),
            P("row"),
            P("col", None, "row"),
            P("col", None, "row"),
            P(),
            P(),
            P(),
            P("row", "col"),
            P("row"),
        ),
        out_specs=P("col", "row"),
        check_vma=False,
    )
```

```python
import math

import jax
import jax.numpy as jnp
import functools

from jax import lax
from jax.experimental import pallas as pl
from jax.sharding import PartitionSpec as P

D = 2048
HD = 128


EPS = 1e-06
THETA = 500000.0
NEG = -1e30


def rotate(states, position):
    half = states.shape[-1] // 2
    freq = THETA ** (-(jnp.arange(half, dtype=jnp.float32) * 2.0 / states.shape[-1]))
    angle = position.astype(jnp.float32)[:, None] * freq[None, :]
    cosine = jnp.cos(angle)
    sine = jnp.sin(angle)
    first = states[..., :half]
    second = states[..., half:]
    return jnp.concatenate(
        [first * cosine - second * sine, second * cosine + first * sine], axis=-1
    )


def group_of(slots, ends):
    return jnp.sum((ends[None, :] <= slots[:, None]).astype(jnp.int32), axis=1)


def butterfly_sum(x, axis, n):
    step = 1
    while step < n:
        x = x + lax.ppermute(x, axis, [(i, i ^ step) for i in range(n)])
        step *= 2
    return x


def halving_scatter(x, axis, n):
    rows = x.shape[0]
    me = lax.axis_index(axis)
    buf = x.reshape(rows, n, x.shape[1] // n)
    step = n // 2
    while step >= 1:
        half = buf.shape[1] // 2
        upper = (me // step) % 2
        keep = lax.dynamic_slice_in_dim(buf, upper * half, half, axis=1)
        send = lax.dynamic_slice_in_dim(buf, (1 - upper) * half, half, axis=1)
        buf = keep + lax.ppermute(send, axis, [(i, i ^ step) for i in range(n)])
        step //= 2
    return buf.reshape(rows, -1)


def doubling_gather(x, axis, n):
    me = lax.axis_index(axis)
    buf = x
    step = 1
    while step < n:
        other = lax.ppermute(buf, axis, [(i, i ^ step) for i in range(n)])
        upper = (me // step) % 2
        lo = jnp.where(upper == 0, buf, other)
        hi = jnp.where(upper == 0, other, buf)
        buf = jnp.concatenate([lo, hi], axis=0)
        step *= 2
    return buf


def partial_kernel(q_ref, qg_ref, qs_ref, k_ref, kg_ref, ks_ref, vt_ref, o_ref, *, scale):
    scores = lax.dot_general(
        k_ref[...], q_ref[...], (((1,), (1,)), ((), ())), preferred_element_type=jnp.float32
    ) * scale
    allowed = (kg_ref[...] == qg_ref[...]) & (ks_ref[...] <= qs_ref[...])
    scores = jnp.where(allowed, scores, NEG)
    top = jnp.max(scores, axis=0, keepdims=True)
    base = jnp.where(top > 0.5 * NEG, top, 0.0)
    weights = jnp.exp(scores - base)
    total = jnp.sum(weights, axis=0, keepdims=True)
    numer = jnp.dot(vt_ref[...], weights.astype(jnp.bfloat16), preferred_element_type=jnp.float32)
    width = o_ref.shape[2]
    hd = vt_ref.shape[0]
    for j in range(o_ref.shape[0]):
        cols = slice(j * width, (j + 1) * width)
        o_ref[j, :hd, :] = numer[:, cols]
        o_ref[j, hd : hd + 1, :] = top[:, cols]
        o_ref[j, hd + 1 : hd + 2, :] = total[:, cols]


def local_partials(queries, q_group, q_slot, keys, k_group, k_slot, values_t, scale, owner_rows, block=256):
    count, hd = queries.shape
    nk = keys.shape[0]
    per = block // owner_rows
    return pl.pallas_call(
        functools.partial(partial_kernel, scale=scale),
        grid=(count // block,),
        in_specs=[
            pl.BlockSpec((block, hd), lambda i: (i, 0)),
            pl.BlockSpec((1, block), lambda i: (0, i)),
            pl.BlockSpec((1, block), lambda i: (0, i)),
            pl.BlockSpec((nk, hd), lambda i: (0, 0)),
            pl.BlockSpec((nk, 1), lambda i: (0, 0)),
            pl.BlockSpec((nk, 1), lambda i: (0, 0)),
            pl.BlockSpec((hd, nk), lambda i: (0, 0)),
        ],
        out_specs=pl.BlockSpec((per, hd + 2, owner_rows), lambda i: (i, 0, 0)),
        out_shape=jax.ShapeDtypeStruct((count // owner_rows, hd + 2, owner_rows), jnp.float32),
        cost_estimate=pl.CostEstimate(
            flops=4 * count * nk * hd, transcendentals=count * nk,
            bytes_accessed=2 * count * hd + 4 * nk * hd + 4 * count * (hd + 2),
        ),
    )(queries, q_group[None, :], q_slot[None, :], keys, k_group[:, None], k_slot[:, None], values_t)


def per_device(
    hidden,
    qkv_weight,
    q_gain,
    k_gain,
    key_cache,
    value_cache,
    page_table,
    suffix_lengths,
    token_slot,
    o_weight,
    norm_gain,
):
    tok_here = hidden.shape[0]
    local_width = q_gain.shape[0]
    group_count = suffix_lengths.shape[0]
    page_size = key_cache.shape[1]
    slots_here = key_cache.shape[0]
    page_total = page_table.shape[0]
    prefix_len = page_total * page_size // group_count
    scale = 1.0 / math.sqrt(HD)
    column = lax.axis_index("col")

    rows_n = D // local_width
    hidden_t = doubling_gather(hidden.T, "row", rows_n)
    weights_here = jnp.concatenate([qkv_weight, o_weight.T[:, None, :]], axis=1)
    weights_all = lax.all_gather(weights_here, "col", axis=0, tiled=True)
    weight_all = weights_all[:, :3]
    out_weight_t = weights_all[:, 3]

    projected = jnp.einsum(
        "dt,dcf->tcf", hidden_t, weight_all, preferred_element_type=jnp.float32
    )
    query_raw = projected[:, 0]
    key_raw = projected[:, 1]
    value_raw = projected[:, 2]
    squares = butterfly_sum(
        jnp.stack([jnp.sum(query_raw * query_raw, axis=1), jnp.sum(key_raw * key_raw, axis=1)]),
        "row",
        rows_n,
    )
    query_norm = query_raw * lax.rsqrt(squares[0] / D + EPS)[:, None] * q_gain
    key_norm = key_raw * lax.rsqrt(squares[1] / D + EPS)[:, None] * k_gain
    ends = jnp.cumsum(suffix_lengths)
    starts = ends - suffix_lengths
    my_slot = lax.dynamic_slice_in_dim(token_slot, column * tok_here, tok_here)
    my_group = group_of(my_slot, ends)
    begin = jnp.sum(
        jnp.where(
            my_group[:, None] == jnp.arange(group_count, dtype=jnp.int32)[None, :],
            starts[None, :],
            0,
        ),
        axis=1,
    )
    position = prefix_len + my_slot - begin
    query_rot = rotate(query_norm, position).astype(jnp.bfloat16)
    key_rot = rotate(key_norm, position).astype(jnp.bfloat16)
    value_here = value_raw.astype(jnp.bfloat16)

    all_query = lax.all_gather(query_rot, "col", axis=0, tiled=True)
    their_group = group_of(token_slot, ends)

    page_slots = column * slots_here + jnp.arange(slots_here, dtype=jnp.int32)
    page_index = jnp.sum(
        jnp.where(
            page_table[None, :] == page_slots[:, None],
            jnp.arange(page_total, dtype=jnp.int32)[None, :],
            0,
        ),
        axis=1,
    )
    slot_group = page_index // (page_total // group_count)
    keys = jnp.concatenate([key_cache.reshape(slots_here * page_size, local_width), key_rot])
    values_t = jnp.concatenate(
        [value_cache.reshape(slots_here * page_size, local_width), value_here]
    ).T
    key_group = jnp.concatenate([jnp.repeat(slot_group, page_size), my_group])
    key_slot = jnp.concatenate([jnp.full((slots_here * page_size,), -1, jnp.int32), my_slot])
    outgoing = local_partials(
        all_query, their_group, token_slot, keys, key_group, key_slot, values_t, scale, tok_here
    )
    incoming = lax.all_to_all(outgoing, "col", split_axis=0, concat_axis=0, tiled=True)
    got_acc = incoming[:, :local_width, :]
    got_top = incoming[:, local_width, :]
    got_sum = incoming[:, local_width + 1, :]
    biggest = jnp.max(got_top, axis=0)
    weight_owner = jnp.exp(got_top - biggest[None])
    denominator = jnp.sum(got_sum * weight_owner, axis=0)
    numerator = jnp.sum(got_acc * weight_owner[:, None, :], axis=0)
    attention_t = (numerator / denominator[None, :]).astype(jnp.bfloat16)
    mixed = jnp.einsum(
        "ht,oh->to", attention_t, out_weight_t, preferred_element_type=jnp.float32
    )
    branch = halving_scatter(mixed, "row", rows_n)
    mean_sq = butterfly_sum(jnp.sum(branch * branch, axis=1), "row", rows_n) / D
    result = hidden.astype(jnp.float32) + branch * lax.rsqrt(mean_sq + EPS)[:, None] * norm_gain
    return result


def solution(mesh):
    return jax.shard_map(
        per_device,
        mesh=mesh,
        in_specs=(
            P("col", "row"),
            P("col", None, "row"),
            P("row"),
            P("row"),
            P("col", None, "row"),
            P("col", None, "row"),
            P(),
            P(),
            P(),
            P("row", "col"),
            P("row"),
        ),
        out_specs=P("col", "row"),
        check_vma=False,
    )
```

```python
import math

import jax
import jax.numpy as jnp
import functools

from jax import lax
from jax.experimental import pallas as pl
from jax.sharding import PartitionSpec as P

D = 2048
HD = 128


EPS = 1e-06
THETA = 500000.0
NEG = -1e30


def rotate(states, position):
    half = states.shape[-1] // 2
    freq = THETA ** (-(jnp.arange(half, dtype=jnp.float32) * 2.0 / states.shape[-1]))
    angle = position.astype(jnp.float32)[:, None] * freq[None, :]
    cosine = jnp.cos(angle)
    sine = jnp.sin(angle)
    first = states[..., :half]
    second = states[..., half:]
    return jnp.concatenate(
        [first * cosine - second * sine, second * cosine + first * sine], axis=-1
    )


def group_of(slots, ends):
    return jnp.sum((ends[None, :] <= slots[:, None]).astype(jnp.int32), axis=1)


def butterfly_sum(x, axis, n):
    step = 1
    while step < n:
        x = x + lax.ppermute(x, axis, [(i, i ^ step) for i in range(n)])
        step *= 2
    return x


def halving_scatter(x, axis, n):
    rows = x.shape[0]
    me = lax.axis_index(axis)
    buf = x.reshape(rows, n, x.shape[1] // n)
    step = n // 2
    while step >= 1:
        half = buf.shape[1] // 2
        upper = (me // step) % 2
        keep = lax.dynamic_slice_in_dim(buf, upper * half, half, axis=1)
        send = lax.dynamic_slice_in_dim(buf, (1 - upper) * half, half, axis=1)
        buf = keep + lax.ppermute(send, axis, [(i, i ^ step) for i in range(n)])
        step //= 2
    return buf.reshape(rows, -1)


def doubling_gather(x, axis, n, order):
    me = lax.axis_index(axis)
    buf = x
    for step in order:
        other = lax.ppermute(buf, axis, [(i, i ^ step) for i in range(n)])
        upper = (me // step) % 2
        lo = jnp.where(upper == 0, buf, other)
        hi = jnp.where(upper == 0, other, buf)
        buf = jnp.concatenate([lo, hi], axis=0)
    bits = [step.bit_length() - 1 for step in order]
    rest = x.shape
    buf = buf.reshape((2,) * len(order) + rest)
    lead = [len(order) - 1 - s for s in range(len(order))]
    by_bit = sorted(range(len(order)), key=lambda s: -bits[s])
    buf = buf.transpose([lead[s] for s in by_bit] + list(range(len(order), len(order) + len(rest))))
    return buf.reshape((n * rest[0],) + rest[1:])


def partial_kernel(q_ref, qg_ref, qs_ref, k_ref, kg_ref, ks_ref, vt_ref, o_ref, *, scale):
    scores = lax.dot_general(
        k_ref[...], q_ref[...], (((1,), (1,)), ((), ())), preferred_element_type=jnp.float32
    ) * scale
    allowed = (kg_ref[...] == qg_ref[...]) & (ks_ref[...] <= qs_ref[...])
    scores = jnp.where(allowed, scores, NEG)
    top = jnp.max(scores, axis=0, keepdims=True)
    base = jnp.where(top > 0.5 * NEG, top, 0.0)
    weights = jnp.exp(scores - base)
    total = jnp.sum(weights, axis=0, keepdims=True)
    numer = jnp.dot(vt_ref[...], weights.astype(jnp.bfloat16), preferred_element_type=jnp.float32)
    width = o_ref.shape[2]
    hd = vt_ref.shape[0]
    for j in range(o_ref.shape[0]):
        cols = slice(j * width, (j + 1) * width)
        o_ref[j, :hd, :] = numer[:, cols]
        o_ref[j, hd : hd + 1, :] = top[:, cols]
        o_ref[j, hd + 1 : hd + 2, :] = total[:, cols]


def local_partials(queries, q_group, q_slot, keys, k_group, k_slot, values_t, scale, owner_rows, block=256):
    count, hd = queries.shape
    nk = keys.shape[0]
    per = block // owner_rows
    return pl.pallas_call(
        functools.partial(partial_kernel, scale=scale),
        grid=(count // block,),
        in_specs=[
            pl.BlockSpec((block, hd), lambda i: (i, 0)),
            pl.BlockSpec((1, block), lambda i: (0, i)),
            pl.BlockSpec((1, block), lambda i: (0, i)),
            pl.BlockSpec((nk, hd), lambda i: (0, 0)),
            pl.BlockSpec((nk, 1), lambda i: (0, 0)),
            pl.BlockSpec((nk, 1), lambda i: (0, 0)),
            pl.BlockSpec((hd, nk), lambda i: (0, 0)),
        ],
        out_specs=pl.BlockSpec((per, hd + 2, owner_rows), lambda i: (i, 0, 0)),
        out_shape=jax.ShapeDtypeStruct((count // owner_rows, hd + 2, owner_rows), jnp.float32),
        cost_estimate=pl.CostEstimate(
            flops=4 * count * nk * hd, transcendentals=count * nk,
            bytes_accessed=2 * count * hd + 4 * nk * hd + 4 * count * (hd + 2),
        ),
    )(queries, q_group[None, :], q_slot[None, :], keys, k_group[:, None], k_slot[:, None], values_t)


def per_device(
    hidden,
    qkv_weight,
    q_gain,
    k_gain,
    key_cache,
    value_cache,
    page_table,
    suffix_lengths,
    token_slot,
    o_weight,
    norm_gain,
):
    tok_here = hidden.shape[0]
    local_width = q_gain.shape[0]
    group_count = suffix_lengths.shape[0]
    page_size = key_cache.shape[1]
    slots_here = key_cache.shape[0]
    page_total = page_table.shape[0]
    prefix_len = page_total * page_size // group_count
    scale = 1.0 / math.sqrt(HD)
    column = lax.axis_index("col")

    rows_n = D // local_width
    cols_n = page_total // slots_here
    row_order = [4, 2, 1, 8] if rows_n == 16 else [1 << i for i in range(rows_n.bit_length() - 1)]
    col_order = [4, 2, 16, 8, 1] if cols_n == 32 else [1 << i for i in range(cols_n.bit_length() - 1)]
    hidden_t = doubling_gather(hidden.T, "row", rows_n, row_order)
    weights_here = jnp.concatenate([qkv_weight, o_weight.T[:, None, :]], axis=1)
    weights_all = doubling_gather(weights_here, "col", cols_n, col_order)
    weight_all = weights_all[:, :3]
    out_weight_t = weights_all[:, 3]

    projected = jnp.einsum(
        "dt,dcf->tcf", hidden_t, weight_all, preferred_element_type=jnp.float32
    )
    query_raw = projected[:, 0]
    key_raw = projected[:, 1]
    value_raw = projected[:, 2]
    squares = butterfly_sum(
        jnp.stack([jnp.sum(query_raw * query_raw, axis=1), jnp.sum(key_raw * key_raw, axis=1)]),
        "row",
        rows_n,
    )
    query_norm = query_raw * lax.rsqrt(squares[0] / D + EPS)[:, None] * q_gain
    key_norm = key_raw * lax.rsqrt(squares[1] / D + EPS)[:, None] * k_gain
    ends = jnp.cumsum(suffix_lengths)
    starts = ends - suffix_lengths
    my_slot = lax.dynamic_slice_in_dim(token_slot, column * tok_here, tok_here)
    my_group = group_of(my_slot, ends)
    begin = jnp.sum(
        jnp.where(
            my_group[:, None] == jnp.arange(group_count, dtype=jnp.int32)[None, :],
            starts[None, :],
            0,
        ),
        axis=1,
    )
    position = prefix_len + my_slot - begin
    query_rot = rotate(query_norm, position).astype(jnp.bfloat16)
    key_rot = rotate(key_norm, position).astype(jnp.bfloat16)
    value_here = value_raw.astype(jnp.bfloat16)

    all_query = doubling_gather(query_rot, "col", cols_n, col_order)
    their_group = group_of(token_slot, ends)

    page_slots = column * slots_here + jnp.arange(slots_here, dtype=jnp.int32)
    page_index = jnp.sum(
        jnp.where(
            page_table[None, :] == page_slots[:, None],
            jnp.arange(page_total, dtype=jnp.int32)[None, :],
            0,
        ),
        axis=1,
    )
    slot_group = page_index // (page_total // group_count)
    keys = jnp.concatenate([key_cache.reshape(slots_here * page_size, local_width), key_rot])
    values_t = jnp.concatenate(
        [value_cache.reshape(slots_here * page_size, local_width), value_here]
    ).T
    key_group = jnp.concatenate([jnp.repeat(slot_group, page_size), my_group])
    key_slot = jnp.concatenate([jnp.full((slots_here * page_size,), -1, jnp.int32), my_slot])
    outgoing = local_partials(
        all_query, their_group, token_slot, keys, key_group, key_slot, values_t, scale, tok_here
    )
    incoming = lax.all_to_all(outgoing, "col", split_axis=0, concat_axis=0, tiled=True)
    got_acc = incoming[:, :local_width, :]
    got_top = incoming[:, local_width, :]
    got_sum = incoming[:, local_width + 1, :]
    biggest = jnp.max(got_top, axis=0)
    weight_owner = jnp.exp(got_top - biggest[None])
    denominator = jnp.sum(got_sum * weight_owner, axis=0)
    numerator = jnp.sum(got_acc * weight_owner[:, None, :], axis=0)
    attention_t = (numerator / denominator[None, :]).astype(jnp.bfloat16)
    mixed = jnp.einsum(
        "ht,oh->to", attention_t, out_weight_t, preferred_element_type=jnp.float32
    )
    branch = halving_scatter(mixed, "row", rows_n)
    mean_sq = butterfly_sum(jnp.sum(branch * branch, axis=1), "row", rows_n) / D
    result = hidden.astype(jnp.float32) + branch * lax.rsqrt(mean_sq + EPS)[:, None] * norm_gain
    return result


def solution(mesh):
    return jax.shard_map(
        per_device,
        mesh=mesh,
        in_specs=(
            P("col", "row"),
            P("col", None, "row"),
            P("row"),
            P("row"),
            P("col", None, "row"),
            P("col", None, "row"),
            P(),
            P(),
            P(),
            P("row", "col"),
            P("row"),
        ),
        out_specs=P("col", "row"),
        check_vma=False,
    )
```

```python
import math

import jax
import jax.numpy as jnp
import functools

from jax import lax
from jax.experimental import pallas as pl
from jax.sharding import PartitionSpec as P

D = 2048
HD = 128


EPS = 1e-06
THETA = 500000.0
NEG = -1e30


def rotate(states, position):
    half = states.shape[-1] // 2
    freq = THETA ** (-(jnp.arange(half, dtype=jnp.float32) * 2.0 / states.shape[-1]))
    angle = position.astype(jnp.float32)[:, None] * freq[None, :]
    cosine = jnp.cos(angle)
    sine = jnp.sin(angle)
    first = states[..., :half]
    second = states[..., half:]
    return jnp.concatenate(
        [first * cosine - second * sine, second * cosine + first * sine], axis=-1
    )


def group_of(slots, ends):
    return jnp.sum((ends[None, :] <= slots[:, None]).astype(jnp.int32), axis=1)


def butterfly_sum(x, axis, n):
    step = 1
    while step < n:
        x = x + lax.ppermute(x, axis, [(i, i ^ step) for i in range(n)])
        step *= 2
    return x


def halving_scatter(x, axis, n):
    rows = x.shape[0]
    me = lax.axis_index(axis)
    buf = x.reshape(rows, n, x.shape[1] // n)
    step = n // 2
    while step >= 1:
        half = buf.shape[1] // 2
        upper = (me // step) % 2
        keep = lax.dynamic_slice_in_dim(buf, upper * half, half, axis=1)
        send = lax.dynamic_slice_in_dim(buf, (1 - upper) * half, half, axis=1)
        buf = keep + lax.ppermute(send, axis, [(i, i ^ step) for i in range(n)])
        step //= 2
    return buf.reshape(rows, -1)


def doubling_gather(x, axis, n, order):
    me = lax.axis_index(axis)
    buf = x
    for step in order:
        other = lax.ppermute(buf, axis, [(i, i ^ step) for i in range(n)])
        upper = (me // step) % 2
        lo = jnp.where(upper == 0, buf, other)
        hi = jnp.where(upper == 0, other, buf)
        buf = jnp.concatenate([lo, hi], axis=0)
    bits = [step.bit_length() - 1 for step in order]
    rest = x.shape
    buf = buf.reshape((2,) * len(order) + rest)
    lead = [len(order) - 1 - s for s in range(len(order))]
    by_bit = sorted(range(len(order)), key=lambda s: -bits[s])
    buf = buf.transpose([lead[s] for s in by_bit] + list(range(len(order), len(order) + len(rest))))
    return buf.reshape((n * rest[0],) + rest[1:])


def partial_kernel(q_ref, qg_ref, qs_ref, k_ref, kg_ref, ks_ref, vt_ref, o_ref, *, scale):
    scores = lax.dot_general(
        k_ref[...], q_ref[...], (((1,), (1,)), ((), ())), preferred_element_type=jnp.float32
    ) * scale
    allowed = (kg_ref[...] == qg_ref[...]) & (ks_ref[...] <= qs_ref[...])
    scores = jnp.where(allowed, scores, NEG)
    top = jnp.max(scores, axis=0, keepdims=True)
    base = jnp.where(top > 0.5 * NEG, top, 0.0)
    weights = jnp.exp(scores - base)
    total = jnp.sum(weights, axis=0, keepdims=True)
    numer = jnp.dot(vt_ref[...], weights.astype(jnp.bfloat16), preferred_element_type=jnp.float32)
    width = o_ref.shape[2]
    hd = vt_ref.shape[0]
    for j in range(o_ref.shape[0]):
        cols = slice(j * width, (j + 1) * width)
        o_ref[j, :hd, :] = numer[:, cols]
        o_ref[j, hd : hd + 1, :] = top[:, cols]
        o_ref[j, hd + 1 : hd + 2, :] = total[:, cols]


def local_partials(queries, q_group, q_slot, keys, k_group, k_slot, values_t, scale, owner_rows, block=256):
    count, hd = queries.shape
    nk = keys.shape[0]
    per = block // owner_rows
    return pl.pallas_call(
        functools.partial(partial_kernel, scale=scale),
        grid=(count // block,),
        in_specs=[
            pl.BlockSpec((block, hd), lambda i: (i, 0)),
            pl.BlockSpec((1, block), lambda i: (0, i)),
            pl.BlockSpec((1, block), lambda i: (0, i)),
            pl.BlockSpec((nk, hd), lambda i: (0, 0)),
            pl.BlockSpec((nk, 1), lambda i: (0, 0)),
            pl.BlockSpec((nk, 1), lambda i: (0, 0)),
            pl.BlockSpec((hd, nk), lambda i: (0, 0)),
        ],
        out_specs=pl.BlockSpec((per, hd + 2, owner_rows), lambda i: (i, 0, 0)),
        out_shape=jax.ShapeDtypeStruct((count // owner_rows, hd + 2, owner_rows), jnp.float32),
        cost_estimate=pl.CostEstimate(
            flops=4 * count * nk * hd, transcendentals=count * nk,
            bytes_accessed=2 * count * hd + 4 * nk * hd + 4 * count * (hd + 2),
        ),
    )(queries, q_group[None, :], q_slot[None, :], keys, k_group[:, None], k_slot[:, None], values_t)


def per_device(
    hidden,
    qkv_weight,
    q_gain,
    k_gain,
    key_cache,
    value_cache,
    page_table,
    suffix_lengths,
    token_slot,
    o_weight,
    norm_gain,
):
    tok_here = hidden.shape[0]
    local_width = q_gain.shape[0]
    group_count = suffix_lengths.shape[0]
    page_size = key_cache.shape[1]
    slots_here = key_cache.shape[0]
    page_total = page_table.shape[0]
    prefix_len = page_total * page_size // group_count
    scale = 1.0 / math.sqrt(HD)
    column = lax.axis_index("col")

    rows_n = D // local_width
    cols_n = page_total // slots_here
    row_order = [4, 2, 1, 8] if rows_n == 16 else [1 << i for i in range(rows_n.bit_length() - 1)]
    col_order = [4, 2, 16, 8, 1] if cols_n == 32 else [1 << i for i in range(cols_n.bit_length() - 1)]
    hidden_t = doubling_gather(hidden.T, "row", rows_n, row_order)
    weight_all = doubling_gather(qkv_weight, "col", cols_n, col_order)
    out_blocks = lax.all_gather(o_weight.T, ("row", "col"), axis=0, tiled=False)

    projected = jnp.einsum(
        "dt,dcf->tcf", hidden_t, weight_all, preferred_element_type=jnp.float32
    )
    query_raw = projected[:, 0]
    key_raw = projected[:, 1]
    value_raw = projected[:, 2]
    squares = butterfly_sum(
        jnp.stack([jnp.sum(query_raw * query_raw, axis=1), jnp.sum(key_raw * key_raw, axis=1)]),
        "row",
        rows_n,
    )
    query_norm = query_raw * lax.rsqrt(squares[0] / D + EPS)[:, None] * q_gain
    key_norm = key_raw * lax.rsqrt(squares[1] / D + EPS)[:, None] * k_gain
    ends = jnp.cumsum(suffix_lengths)
    starts = ends - suffix_lengths
    my_slot = lax.dynamic_slice_in_dim(token_slot, column * tok_here, tok_here)
    my_group = group_of(my_slot, ends)
    begin = jnp.sum(
        jnp.where(
            my_group[:, None] == jnp.arange(group_count, dtype=jnp.int32)[None, :],
            starts[None, :],
            0,
        ),
        axis=1,
    )
    position = prefix_len + my_slot - begin
    query_rot = rotate(query_norm, position).astype(jnp.bfloat16)
    key_rot = rotate(key_norm, position).astype(jnp.bfloat16)
    value_here = value_raw.astype(jnp.bfloat16)

    all_query = doubling_gather(query_rot, "col", cols_n, col_order)
    their_group = group_of(token_slot, ends)

    page_slots = column * slots_here + jnp.arange(slots_here, dtype=jnp.int32)
    page_index = jnp.sum(
        jnp.where(
            page_table[None, :] == page_slots[:, None],
            jnp.arange(page_total, dtype=jnp.int32)[None, :],
            0,
        ),
        axis=1,
    )
    slot_group = page_index // (page_total // group_count)
    keys = jnp.concatenate([key_cache.reshape(slots_here * page_size, local_width), key_rot])
    values_t = jnp.concatenate(
        [value_cache.reshape(slots_here * page_size, local_width), value_here]
    ).T
    key_group = jnp.concatenate([jnp.repeat(slot_group, page_size), my_group])
    key_slot = jnp.concatenate([jnp.full((slots_here * page_size,), -1, jnp.int32), my_slot])
    outgoing = local_partials(
        all_query, their_group, token_slot, keys, key_group, key_slot, values_t, scale, tok_here
    )
    incoming = lax.all_to_all(outgoing, "col", split_axis=0, concat_axis=0, tiled=True)
    got_acc = incoming[:, :local_width, :]
    got_top = incoming[:, local_width, :]
    got_sum = incoming[:, local_width + 1, :]
    biggest = jnp.max(got_top, axis=0)
    weight_owner = jnp.exp(got_top - biggest[None])
    denominator = jnp.sum(got_sum * weight_owner, axis=0)
    numerator = jnp.sum(got_acc * weight_owner[:, None, :], axis=0)
    attention_t = (numerator / denominator[None, :]).astype(jnp.bfloat16)
    heads_all = doubling_gather(attention_t, "row", rows_n, row_order)
    head_rows = o_weight.shape[0]
    mixed = jnp.einsum(
        "rht,rcoh->tco",
        heads_all.reshape(rows_n, head_rows, tok_here),
        out_blocks.reshape(rows_n, cols_n, o_weight.shape[1], head_rows),
        preferred_element_type=jnp.float32,
    ).reshape(tok_here, D)
    mean_sq = jnp.mean(mixed * mixed, axis=1)
    branch = lax.dynamic_slice_in_dim(mixed, lax.axis_index("row") * local_width, local_width, axis=1)
    result = hidden.astype(jnp.float32) + branch * lax.rsqrt(mean_sq + EPS)[:, None] * norm_gain
    return result


def solution(mesh):
    return jax.shard_map(
        per_device,
        mesh=mesh,
        in_specs=(
            P("col", "row"),
            P("col", None, "row"),
            P("row"),
            P("row"),
            P("col", None, "row"),
            P("col", None, "row"),
            P(),
            P(),
            P(),
            P("row", "col"),
            P("row"),
        ),
        out_specs=P("col", "row"),
        check_vma=False,
    )
```

```python
import math

import jax
import jax.numpy as jnp
import functools

from jax import lax
from jax.experimental import pallas as pl
from jax.sharding import PartitionSpec as P

D = 2048
HD = 128


EPS = 1e-06
THETA = 500000.0
NEG = -1e30


def rotate(states, position):
    half = states.shape[-1] // 2
    freq = THETA ** (-(jnp.arange(half, dtype=jnp.float32) * 2.0 / states.shape[-1]))
    angle = position.astype(jnp.float32)[:, None] * freq[None, :]
    cosine = jnp.cos(angle)
    sine = jnp.sin(angle)
    first = states[..., :half]
    second = states[..., half:]
    return jnp.concatenate(
        [first * cosine - second * sine, second * cosine + first * sine], axis=-1
    )


def group_of(slots, ends):
    return jnp.sum((ends[None, :] <= slots[:, None]).astype(jnp.int32), axis=1)


def butterfly_sum(x, axis, n):
    step = 1
    while step < n:
        x = x + lax.ppermute(x, axis, [(i, i ^ step) for i in range(n)])
        step *= 2
    return x


def halving_scatter(x, axis, n):
    rows = x.shape[0]
    me = lax.axis_index(axis)
    buf = x.reshape(rows, n, x.shape[1] // n)
    step = n // 2
    while step >= 1:
        half = buf.shape[1] // 2
        upper = (me // step) % 2
        keep = lax.dynamic_slice_in_dim(buf, upper * half, half, axis=1)
        send = lax.dynamic_slice_in_dim(buf, (1 - upper) * half, half, axis=1)
        buf = keep + lax.ppermute(send, axis, [(i, i ^ step) for i in range(n)])
        step //= 2
    return buf.reshape(rows, -1)


def doubling_gather(x, axis, n, order):
    me = lax.axis_index(axis)
    buf = x
    for step in order:
        other = lax.ppermute(buf, axis, [(i, i ^ step) for i in range(n)])
        upper = (me // step) % 2
        lo = jnp.where(upper == 0, buf, other)
        hi = jnp.where(upper == 0, other, buf)
        buf = jnp.concatenate([lo, hi], axis=0)
    bits = [step.bit_length() - 1 for step in order]
    rest = x.shape
    buf = buf.reshape((2,) * len(order) + rest)
    lead = [len(order) - 1 - s for s in range(len(order))]
    by_bit = sorted(range(len(order)), key=lambda s: -bits[s])
    buf = buf.transpose([lead[s] for s in by_bit] + list(range(len(order), len(order) + len(rest))))
    return buf.reshape((n * rest[0],) + rest[1:])


def partial_kernel(q_ref, qg_ref, qs_ref, k_ref, kg_ref, ks_ref, vt_ref, o_ref, *, scale):
    scores = lax.dot_general(
        k_ref[...], q_ref[...], (((1,), (1,)), ((), ())), preferred_element_type=jnp.float32
    ) * scale
    allowed = (kg_ref[...] == qg_ref[...]) & (ks_ref[...] <= qs_ref[...])
    scores = jnp.where(allowed, scores, NEG)
    top = jnp.max(scores, axis=0, keepdims=True)
    base = jnp.where(top > 0.5 * NEG, top, 0.0)
    weights = jnp.exp(scores - base)
    total = jnp.sum(weights, axis=0, keepdims=True)
    numer = jnp.dot(vt_ref[...], weights.astype(jnp.bfloat16), preferred_element_type=jnp.float32)
    width = o_ref.shape[2]
    hd = vt_ref.shape[0]
    for j in range(o_ref.shape[0]):
        cols = slice(j * width, (j + 1) * width)
        o_ref[j, :hd, :] = numer[:, cols]
        o_ref[j, hd : hd + 1, :] = top[:, cols]
        o_ref[j, hd + 1 : hd + 2, :] = total[:, cols]


def local_partials(queries, q_group, q_slot, keys, k_group, k_slot, values_t, scale, owner_rows, block=256):
    count, hd = queries.shape
    nk = keys.shape[0]
    per = block // owner_rows
    return pl.pallas_call(
        functools.partial(partial_kernel, scale=scale),
        grid=(count // block,),
        in_specs=[
            pl.BlockSpec((block, hd), lambda i: (i, 0)),
            pl.BlockSpec((1, block), lambda i: (0, i)),
            pl.BlockSpec((1, block), lambda i: (0, i)),
            pl.BlockSpec((nk, hd), lambda i: (0, 0)),
            pl.BlockSpec((nk, 1), lambda i: (0, 0)),
            pl.BlockSpec((nk, 1), lambda i: (0, 0)),
            pl.BlockSpec((hd, nk), lambda i: (0, 0)),
        ],
        out_specs=pl.BlockSpec((per, hd + 2, owner_rows), lambda i: (i, 0, 0)),
        out_shape=jax.ShapeDtypeStruct((count // owner_rows, hd + 2, owner_rows), jnp.float32),
        cost_estimate=pl.CostEstimate(
            flops=4 * count * nk * hd, transcendentals=count * nk,
            bytes_accessed=2 * count * hd + 4 * nk * hd + 4 * count * (hd + 2),
        ),
    )(queries, q_group[None, :], q_slot[None, :], keys, k_group[:, None], k_slot[:, None], values_t)


def per_device(
    hidden,
    qkv_weight,
    q_gain,
    k_gain,
    key_cache,
    value_cache,
    page_table,
    suffix_lengths,
    token_slot,
    o_weight,
    norm_gain,
):
    tok_here = hidden.shape[0]
    local_width = q_gain.shape[0]
    group_count = suffix_lengths.shape[0]
    page_size = key_cache.shape[1]
    slots_here = key_cache.shape[0]
    page_total = page_table.shape[0]
    prefix_len = page_total * page_size // group_count
    scale = 1.0 / math.sqrt(HD)
    column = lax.axis_index("col")

    rows_n = D // local_width
    cols_n = page_total // slots_here
    row_order = [4, 2, 1, 8] if rows_n == 16 else [1 << i for i in range(rows_n.bit_length() - 1)]
    col_order = [4, 2, 16, 8, 1] if cols_n == 32 else [1 << i for i in range(cols_n.bit_length() - 1)]
    hidden_t = doubling_gather(hidden.T, "row", rows_n, row_order)
    weight_all = doubling_gather(qkv_weight, "col", cols_n, col_order)
    out_rows = doubling_gather(o_weight, "row", rows_n, row_order)
    out_weight_t = lax.all_gather(out_rows.T, "col", axis=0, tiled=True)

    projected = jnp.einsum(
        "dt,dcf->tcf", hidden_t, weight_all, preferred_element_type=jnp.float32
    )
    query_raw = projected[:, 0]
    key_raw = projected[:, 1]
    value_raw = projected[:, 2]
    squares = butterfly_sum(
        jnp.stack([jnp.sum(query_raw * query_raw, axis=1), jnp.sum(key_raw * key_raw, axis=1)]),
        "row",
        rows_n,
    )
    query_norm = query_raw * lax.rsqrt(squares[0] / D + EPS)[:, None] * q_gain
    key_norm = key_raw * lax.rsqrt(squares[1] / D + EPS)[:, None] * k_gain
    ends = jnp.cumsum(suffix_lengths)
    starts = ends - suffix_lengths
    my_slot = lax.dynamic_slice_in_dim(token_slot, column * tok_here, tok_here)
    my_group = group_of(my_slot, ends)
    begin = jnp.sum(
        jnp.where(
            my_group[:, None] == jnp.arange(group_count, dtype=jnp.int32)[None, :],
            starts[None, :],
            0,
        ),
        axis=1,
    )
    position = prefix_len + my_slot - begin
    query_rot = rotate(query_norm, position).astype(jnp.bfloat16)
    key_rot = rotate(key_norm, position).astype(jnp.bfloat16)
    value_here = value_raw.astype(jnp.bfloat16)

    all_query = doubling_gather(query_rot, "col", cols_n, col_order)
    their_group = group_of(token_slot, ends)

    page_slots = column * slots_here + jnp.arange(slots_here, dtype=jnp.int32)
    page_index = jnp.sum(
        jnp.where(
            page_table[None, :] == page_slots[:, None],
            jnp.arange(page_total, dtype=jnp.int32)[None, :],
            0,
        ),
        axis=1,
    )
    slot_group = page_index // (page_total // group_count)
    keys = jnp.concatenate([key_cache.reshape(slots_here * page_size, local_width), key_rot])
    values_t = jnp.concatenate(
        [value_cache.reshape(slots_here * page_size, local_width), value_here]
    ).T
    key_group = jnp.concatenate([jnp.repeat(slot_group, page_size), my_group])
    key_slot = jnp.concatenate([jnp.full((slots_here * page_size,), -1, jnp.int32), my_slot])
    outgoing = local_partials(
        all_query, their_group, token_slot, keys, key_group, key_slot, values_t, scale, tok_here
    )
    incoming = lax.all_to_all(outgoing, "col", split_axis=0, concat_axis=0, tiled=True)
    got_acc = incoming[:, :local_width, :]
    got_top = incoming[:, local_width, :]
    got_sum = incoming[:, local_width + 1, :]
    biggest = jnp.max(got_top, axis=0)
    weight_owner = jnp.exp(got_top - biggest[None])
    denominator = jnp.sum(got_sum * weight_owner, axis=0)
    numerator = jnp.sum(got_acc * weight_owner[:, None, :], axis=0)
    attention_t = (numerator / denominator[None, :]).astype(jnp.bfloat16)
    heads_all = doubling_gather(attention_t, "row", rows_n, row_order)
    mixed = jnp.dot(heads_all.T, out_weight_t.T, preferred_element_type=jnp.float32)
    mean_sq = jnp.mean(mixed * mixed, axis=1)
    branch = lax.dynamic_slice_in_dim(mixed, lax.axis_index("row") * local_width, local_width, axis=1)
    result = hidden.astype(jnp.float32) + branch * lax.rsqrt(mean_sq + EPS)[:, None] * norm_gain
    return result


def solution(mesh):
    return jax.shard_map(
        per_device,
        mesh=mesh,
        in_specs=(
            P("col", "row"),
            P("col", None, "row"),
            P("row"),
            P("row"),
            P("col", None, "row"),
            P("col", None, "row"),
            P(),
            P(),
            P(),
            P("row", "col"),
            P("row"),
        ),
        out_specs=P("col", "row"),
        check_vma=False,
    )
```

```python
import math

import jax
import jax.numpy as jnp
import functools

from jax import lax
from jax.experimental import pallas as pl
from jax.sharding import PartitionSpec as P

D = 2048
HD = 128


EPS = 1e-06
THETA = 500000.0
NEG = -1e30


def rotate(states, position):
    half = states.shape[-1] // 2
    freq = THETA ** (-(jnp.arange(half, dtype=jnp.float32) * 2.0 / states.shape[-1]))
    angle = position.astype(jnp.float32)[:, None] * freq[None, :]
    cosine = jnp.cos(angle)
    sine = jnp.sin(angle)
    first = states[..., :half]
    second = states[..., half:]
    return jnp.concatenate(
        [first * cosine - second * sine, second * cosine + first * sine], axis=-1
    )


def group_of(slots, ends):
    return jnp.sum((ends[None, :] <= slots[:, None]).astype(jnp.int32), axis=1)


def butterfly_sum(x, axis, n):
    step = 1
    while step < n:
        x = x + lax.ppermute(x, axis, [(i, i ^ step) for i in range(n)])
        step *= 2
    return x


def halving_scatter(x, axis, n):
    rows = x.shape[0]
    me = lax.axis_index(axis)
    buf = x.reshape(rows, n, x.shape[1] // n)
    step = n // 2
    while step >= 1:
        half = buf.shape[1] // 2
        upper = (me // step) % 2
        keep = lax.dynamic_slice_in_dim(buf, upper * half, half, axis=1)
        send = lax.dynamic_slice_in_dim(buf, (1 - upper) * half, half, axis=1)
        buf = keep + lax.ppermute(send, axis, [(i, i ^ step) for i in range(n)])
        step //= 2
    return buf.reshape(rows, -1)


def doubling_gather(x, axis, n, order):
    me = lax.axis_index(axis)
    buf = x
    for step in order:
        other = lax.ppermute(buf, axis, [(i, i ^ step) for i in range(n)])
        upper = (me // step) % 2
        lo = jnp.where(upper == 0, buf, other)
        hi = jnp.where(upper == 0, other, buf)
        buf = jnp.concatenate([lo, hi], axis=0)
    bits = [step.bit_length() - 1 for step in order]
    rest = x.shape
    buf = buf.reshape((2,) * len(order) + rest)
    lead = [len(order) - 1 - s for s in range(len(order))]
    by_bit = sorted(range(len(order)), key=lambda s: -bits[s])
    buf = buf.transpose([lead[s] for s in by_bit] + list(range(len(order), len(order) + len(rest))))
    return buf.reshape((n * rest[0],) + rest[1:])


def partial_kernel(q_ref, qg_ref, qs_ref, k_ref, kg_ref, ks_ref, vt_ref, o_ref, *, scale):
    scores = lax.dot_general(
        k_ref[...], q_ref[...], (((1,), (1,)), ((), ())), preferred_element_type=jnp.float32
    ) * scale
    allowed = (kg_ref[...] == qg_ref[...]) & (ks_ref[...] <= qs_ref[...])
    scores = jnp.where(allowed, scores, NEG)
    top = jnp.max(scores, axis=0, keepdims=True)
    base = jnp.where(top > 0.5 * NEG, top, 0.0)
    weights = jnp.exp(scores - base)
    total = jnp.sum(weights, axis=0, keepdims=True)
    numer = jnp.dot(vt_ref[...], weights.astype(jnp.bfloat16), preferred_element_type=jnp.float32)
    width = o_ref.shape[2]
    hd = vt_ref.shape[0]
    for j in range(o_ref.shape[0]):
        cols = slice(j * width, (j + 1) * width)
        o_ref[j, :hd, :] = numer[:, cols]
        o_ref[j, hd : hd + 1, :] = top[:, cols]
        o_ref[j, hd + 1 : hd + 2, :] = total[:, cols]


def local_partials(queries, q_group, q_slot, keys, k_group, k_slot, values_t, scale, owner_rows, block=512):
    count, hd = queries.shape
    nk = keys.shape[0]
    per = block // owner_rows
    return pl.pallas_call(
        functools.partial(partial_kernel, scale=scale),
        grid=(count // block,),
        in_specs=[
            pl.BlockSpec((block, hd), lambda i: (i, 0)),
            pl.BlockSpec((1, block), lambda i: (0, i)),
            pl.BlockSpec((1, block), lambda i: (0, i)),
            pl.BlockSpec((nk, hd), lambda i: (0, 0)),
            pl.BlockSpec((nk, 1), lambda i: (0, 0)),
            pl.BlockSpec((nk, 1), lambda i: (0, 0)),
            pl.BlockSpec((hd, nk), lambda i: (0, 0)),
        ],
        out_specs=pl.BlockSpec((per, hd + 2, owner_rows), lambda i: (i, 0, 0)),
        out_shape=jax.ShapeDtypeStruct((count // owner_rows, hd + 2, owner_rows), jnp.float32),
        cost_estimate=pl.CostEstimate(
            flops=4 * count * nk * hd, transcendentals=count * nk,
            bytes_accessed=2 * count * hd + 4 * nk * hd + 4 * count * (hd + 2),
        ),
    )(queries, q_group[None, :], q_slot[None, :], keys, k_group[:, None], k_slot[:, None], values_t)


def per_device(
    hidden,
    qkv_weight,
    q_gain,
    k_gain,
    key_cache,
    value_cache,
    page_table,
    suffix_lengths,
    token_slot,
    o_weight,
    norm_gain,
):
    tok_here = hidden.shape[0]
    local_width = q_gain.shape[0]
    group_count = suffix_lengths.shape[0]
    page_size = key_cache.shape[1]
    slots_here = key_cache.shape[0]
    page_total = page_table.shape[0]
    prefix_len = page_total * page_size // group_count
    scale = 1.0 / math.sqrt(HD)
    column = lax.axis_index("col")

    rows_n = D // local_width
    cols_n = page_total // slots_here
    row_order = [4, 2, 1, 8] if rows_n == 16 else [1 << i for i in range(rows_n.bit_length() - 1)]
    col_order = [4, 2, 16, 8, 1] if cols_n == 32 else [1 << i for i in range(cols_n.bit_length() - 1)]
    hidden_t = doubling_gather(hidden.T, "row", rows_n, row_order)
    weight_all = doubling_gather(qkv_weight, "col", cols_n, col_order)
    out_rows = doubling_gather(o_weight, "row", rows_n, row_order)
    out_weight_t = doubling_gather(out_rows.T, "col", cols_n, col_order)

    projected = jnp.einsum(
        "dt,dcf->tcf", hidden_t, weight_all, preferred_element_type=jnp.float32
    )
    query_raw = projected[:, 0]
    key_raw = projected[:, 1]
    value_raw = projected[:, 2]
    squares = butterfly_sum(
        jnp.stack([jnp.sum(query_raw * query_raw, axis=1), jnp.sum(key_raw * key_raw, axis=1)]),
        "row",
        rows_n,
    )
    query_norm = query_raw * lax.rsqrt(squares[0] / D + EPS)[:, None] * q_gain
    key_norm = key_raw * lax.rsqrt(squares[1] / D + EPS)[:, None] * k_gain
    ends = jnp.cumsum(suffix_lengths)
    starts = ends - suffix_lengths
    my_slot = lax.dynamic_slice_in_dim(token_slot, column * tok_here, tok_here)
    my_group = group_of(my_slot, ends)
    begin = jnp.sum(
        jnp.where(
            my_group[:, None] == jnp.arange(group_count, dtype=jnp.int32)[None, :],
            starts[None, :],
            0,
        ),
        axis=1,
    )
    position = prefix_len + my_slot - begin
    query_rot = rotate(query_norm, position).astype(jnp.bfloat16)
    key_rot = rotate(key_norm, position).astype(jnp.bfloat16)
    value_here = value_raw.astype(jnp.bfloat16)

    all_query = doubling_gather(query_rot, "col", cols_n, col_order)
    their_group = group_of(token_slot, ends)

    page_slots = column * slots_here + jnp.arange(slots_here, dtype=jnp.int32)
    page_index = jnp.sum(
        jnp.where(
            page_table[None, :] == page_slots[:, None],
            jnp.arange(page_total, dtype=jnp.int32)[None, :],
            0,
        ),
        axis=1,
    )
    slot_group = page_index // (page_total // group_count)
    keys = jnp.concatenate([key_cache.reshape(slots_here * page_size, local_width), key_rot])
    values_t = jnp.concatenate(
        [value_cache.reshape(slots_here * page_size, local_width), value_here]
    ).T
    key_group = jnp.concatenate([jnp.repeat(slot_group, page_size), my_group])
    key_slot = jnp.concatenate([jnp.full((slots_here * page_size,), -1, jnp.int32), my_slot])
    outgoing = local_partials(
        all_query, their_group, token_slot, keys, key_group, key_slot, values_t, scale, tok_here
    )
    incoming = lax.all_to_all(outgoing, "col", split_axis=0, concat_axis=0, tiled=True)
    got_acc = incoming[:, :local_width, :]
    got_top = incoming[:, local_width, :]
    got_sum = incoming[:, local_width + 1, :]
    biggest = jnp.max(got_top, axis=0)
    weight_owner = jnp.exp(got_top - biggest[None])
    denominator = jnp.sum(got_sum * weight_owner, axis=0)
    numerator = jnp.sum(got_acc * weight_owner[:, None, :], axis=0)
    attention_t = (numerator / denominator[None, :]).astype(jnp.bfloat16)
    heads_all = doubling_gather(attention_t, "row", rows_n, row_order)
    mixed = jnp.dot(heads_all.T, out_weight_t.T, preferred_element_type=jnp.float32)
    mean_sq = jnp.mean(mixed * mixed, axis=1)
    branch = lax.dynamic_slice_in_dim(mixed, lax.axis_index("row") * local_width, local_width, axis=1)
    result = hidden.astype(jnp.float32) + branch * lax.rsqrt(mean_sq + EPS)[:, None] * norm_gain
    return result


def solution(mesh):
    return jax.shard_map(
        per_device,
        mesh=mesh,
        in_specs=(
            P("col", "row"),
            P("col", None, "row"),
            P("row"),
            P("row"),
            P("col", None, "row"),
            P("col", None, "row"),
            P(),
            P(),
            P(),
            P("row", "col"),
            P("row"),
        ),
        out_specs=P("col", "row"),
        check_vma=False,
    )
```

```python
import math

import jax
import jax.numpy as jnp
import functools

from jax import lax
from jax.experimental import pallas as pl
from jax.sharding import PartitionSpec as P

D = 2048
HD = 128


EPS = 1e-06
THETA = 500000.0
NEG = -1e30


def rotate(states, position):
    half = states.shape[-1] // 2
    freq = THETA ** (-(jnp.arange(half, dtype=jnp.float32) * 2.0 / states.shape[-1]))
    angle = position.astype(jnp.float32)[:, None] * freq[None, :]
    cosine = jnp.cos(angle)
    sine = jnp.sin(angle)
    first = states[..., :half]
    second = states[..., half:]
    return jnp.concatenate(
        [first * cosine - second * sine, second * cosine + first * sine], axis=-1
    )


def group_of(slots, ends):
    return jnp.sum((ends[None, :] <= slots[:, None]).astype(jnp.int32), axis=1)


def butterfly_sum(x, axis, n):
    step = 1
    while step < n:
        x = x + lax.ppermute(x, axis, [(i, i ^ step) for i in range(n)])
        step *= 2
    return x


def halving_scatter(x, axis, n):
    rows = x.shape[0]
    me = lax.axis_index(axis)
    buf = x.reshape(rows, n, x.shape[1] // n)
    step = n // 2
    while step >= 1:
        half = buf.shape[1] // 2
        upper = (me // step) % 2
        keep = lax.dynamic_slice_in_dim(buf, upper * half, half, axis=1)
        send = lax.dynamic_slice_in_dim(buf, (1 - upper) * half, half, axis=1)
        buf = keep + lax.ppermute(send, axis, [(i, i ^ step) for i in range(n)])
        step //= 2
    return buf.reshape(rows, -1)


def doubling_gather(x, axis, n, order):
    me = lax.axis_index(axis)
    buf = x
    for step in order:
        other = lax.ppermute(buf, axis, [(i, i ^ step) for i in range(n)])
        upper = (me // step) % 2
        lo = jnp.where(upper == 0, buf, other)
        hi = jnp.where(upper == 0, other, buf)
        buf = jnp.concatenate([lo, hi], axis=0)
    bits = [step.bit_length() - 1 for step in order]
    rest = x.shape
    buf = buf.reshape((2,) * len(order) + rest)
    lead = [len(order) - 1 - s for s in range(len(order))]
    by_bit = sorted(range(len(order)), key=lambda s: -bits[s])
    buf = buf.transpose([lead[s] for s in by_bit] + list(range(len(order), len(order) + len(rest))))
    return buf.reshape((n * rest[0],) + rest[1:])


def partial_kernel(q_ref, qg_ref, qs_ref, k_ref, kg_ref, ks_ref, vt_ref, o_ref, *, scale):
    scores = lax.dot_general(
        k_ref[...], q_ref[...], (((1,), (1,)), ((), ())), preferred_element_type=jnp.float32
    ) * scale
    allowed = (kg_ref[...] == qg_ref[...]) & (ks_ref[...] <= qs_ref[...])
    scores = jnp.where(allowed, scores, NEG)
    top = jnp.max(scores, axis=0, keepdims=True)
    top_hi = top.astype(jnp.bfloat16).astype(jnp.float32)
    top_lo = (top - top_hi).astype(jnp.bfloat16).astype(jnp.float32)
    base = jnp.where(top > 0.5 * NEG, top_hi + top_lo, 0.0)
    weights = jnp.exp(scores - base)
    total = jnp.sum(weights, axis=0, keepdims=True)
    total_hi = total.astype(jnp.bfloat16).astype(jnp.float32)
    total_lo = (total - total_hi).astype(jnp.bfloat16).astype(jnp.float32)
    numer = jnp.dot(vt_ref[...], weights.astype(jnp.bfloat16), preferred_element_type=jnp.float32)
    width = o_ref.shape[2]
    hd = vt_ref.shape[0]
    extra = o_ref.shape[1] - hd
    row = lax.broadcasted_iota(jnp.int32, (extra, top.shape[1]), 0)
    stats = jnp.where(
        row == 0, top_hi, jnp.where(row == 1, top_lo, jnp.where(row == 2, total_hi, jnp.where(row == 3, total_lo, 0.0)))
    )
    for j in range(o_ref.shape[0]):
        cols = slice(j * width, (j + 1) * width)
        o_ref[j, :hd, :] = numer[:, cols].astype(o_ref.dtype)
        o_ref[j, hd:, :] = stats[:, cols].astype(o_ref.dtype)


def local_partials(queries, q_group, q_slot, keys, k_group, k_slot, values_t, scale, owner_rows, block=512):
    count, hd = queries.shape
    nk = keys.shape[0]
    per = block // owner_rows
    return pl.pallas_call(
        functools.partial(partial_kernel, scale=scale),
        grid=(count // block,),
        in_specs=[
            pl.BlockSpec((block, hd), lambda i: (i, 0)),
            pl.BlockSpec((1, block), lambda i: (0, i)),
            pl.BlockSpec((1, block), lambda i: (0, i)),
            pl.BlockSpec((nk, hd), lambda i: (0, 0)),
            pl.BlockSpec((nk, 1), lambda i: (0, 0)),
            pl.BlockSpec((nk, 1), lambda i: (0, 0)),
            pl.BlockSpec((hd, nk), lambda i: (0, 0)),
        ],
        out_specs=pl.BlockSpec((per, hd + 16, owner_rows), lambda i: (i, 0, 0)),
        out_shape=jax.ShapeDtypeStruct((count // owner_rows, hd + 16, owner_rows), jnp.bfloat16),
        cost_estimate=pl.CostEstimate(
            flops=4 * count * nk * hd, transcendentals=count * nk,
            bytes_accessed=2 * count * hd + 4 * nk * hd + 2 * count * (hd + 16),
        ),
    )(queries, q_group[None, :], q_slot[None, :], keys, k_group[:, None], k_slot[:, None], values_t)


def per_device(
    hidden,
    qkv_weight,
    q_gain,
    k_gain,
    key_cache,
    value_cache,
    page_table,
    suffix_lengths,
    token_slot,
    o_weight,
    norm_gain,
):
    tok_here = hidden.shape[0]
    local_width = q_gain.shape[0]
    group_count = suffix_lengths.shape[0]
    page_size = key_cache.shape[1]
    slots_here = key_cache.shape[0]
    page_total = page_table.shape[0]
    prefix_len = page_total * page_size // group_count
    scale = 1.0 / math.sqrt(HD)
    column = lax.axis_index("col")

    rows_n = D // local_width
    cols_n = page_total // slots_here
    row_order = [4, 2, 1, 8] if rows_n == 16 else [1 << i for i in range(rows_n.bit_length() - 1)]
    col_order = [4, 2, 16, 8, 1] if cols_n == 32 else [1 << i for i in range(cols_n.bit_length() - 1)]
    hidden_t = doubling_gather(hidden.T, "row", rows_n, row_order)
    weight_all = doubling_gather(qkv_weight, "col", cols_n, col_order)
    out_rows = doubling_gather(o_weight, "row", rows_n, row_order)
    out_weight_t = lax.all_gather(out_rows.T, "col", axis=0, tiled=True)

    projected = jnp.einsum(
        "dt,dcf->tcf", hidden_t, weight_all, preferred_element_type=jnp.float32
    )
    query_raw = projected[:, 0]
    key_raw = projected[:, 1]
    value_raw = projected[:, 2]
    squares = butterfly_sum(
        jnp.stack([jnp.sum(query_raw * query_raw, axis=1), jnp.sum(key_raw * key_raw, axis=1)]),
        "row",
        rows_n,
    )
    query_norm = query_raw * lax.rsqrt(squares[0] / D + EPS)[:, None] * q_gain
    key_norm = key_raw * lax.rsqrt(squares[1] / D + EPS)[:, None] * k_gain
    ends = jnp.cumsum(suffix_lengths)
    starts = ends - suffix_lengths
    my_slot = lax.dynamic_slice_in_dim(token_slot, column * tok_here, tok_here)
    my_group = group_of(my_slot, ends)
    begin = jnp.sum(
        jnp.where(
            my_group[:, None] == jnp.arange(group_count, dtype=jnp.int32)[None, :],
            starts[None, :],
            0,
        ),
        axis=1,
    )
    position = prefix_len + my_slot - begin
    query_rot = rotate(query_norm, position).astype(jnp.bfloat16)
    key_rot = rotate(key_norm, position).astype(jnp.bfloat16)
    value_here = value_raw.astype(jnp.bfloat16)

    all_query = doubling_gather(query_rot, "col", cols_n, col_order)
    their_group = group_of(token_slot, ends)

    page_slots = column * slots_here + jnp.arange(slots_here, dtype=jnp.int32)
    page_index = jnp.sum(
        jnp.where(
            page_table[None, :] == page_slots[:, None],
            jnp.arange(page_total, dtype=jnp.int32)[None, :],
            0,
        ),
        axis=1,
    )
    slot_group = page_index // (page_total // group_count)
    keys = jnp.concatenate([key_cache.reshape(slots_here * page_size, local_width), key_rot])
    values_t = jnp.concatenate(
        [value_cache.reshape(slots_here * page_size, local_width), value_here]
    ).T
    key_group = jnp.concatenate([jnp.repeat(slot_group, page_size), my_group])
    key_slot = jnp.concatenate([jnp.full((slots_here * page_size,), -1, jnp.int32), my_slot])
    outgoing = local_partials(
        all_query, their_group, token_slot, keys, key_group, key_slot, values_t, scale, tok_here
    )
    incoming = lax.all_to_all(outgoing, "col", split_axis=0, concat_axis=0, tiled=True)
    got_acc = incoming[:, :local_width, :].astype(jnp.float32)
    halves = incoming[:, local_width : local_width + 4, :].astype(jnp.float32)
    got_top = halves[:, 0] + halves[:, 1]
    got_sum = halves[:, 2] + halves[:, 3]
    biggest = jnp.max(got_top, axis=0)
    weight_owner = jnp.exp(got_top - biggest[None])
    denominator = jnp.sum(got_sum * weight_owner, axis=0)
    numerator = jnp.sum(got_acc * weight_owner[:, None, :], axis=0)
    attention_t = (numerator / denominator[None, :]).astype(jnp.bfloat16)
    heads_all = doubling_gather(attention_t, "row", rows_n, row_order)
    mixed = jnp.dot(heads_all.T, out_weight_t.T, preferred_element_type=jnp.float32)
    mean_sq = jnp.mean(mixed * mixed, axis=1)
    branch = lax.dynamic_slice_in_dim(mixed, lax.axis_index("row") * local_width, local_width, axis=1)
    result = hidden.astype(jnp.float32) + branch * lax.rsqrt(mean_sq + EPS)[:, None] * norm_gain
    return result


def solution(mesh):
    return jax.shard_map(
        per_device,
        mesh=mesh,
        in_specs=(
            P("col", "row"),
            P("col", None, "row"),
            P("row"),
            P("row"),
            P("col", None, "row"),
            P("col", None, "row"),
            P(),
            P(),
            P(),
            P("row", "col"),
            P("row"),
        ),
        out_specs=P("col", "row"),
        check_vma=False,
    )
```

```python
import math

import jax
import jax.numpy as jnp
import functools

from jax import lax
from jax.experimental import pallas as pl
from jax.experimental.pallas import tpu as pltpu
from jax.sharding import PartitionSpec as P

D = 2048
HD = 128


EPS = 1e-06
THETA = 500000.0
NEG = -1e30


def rotate(states, position):
    half = states.shape[-1] // 2
    freq = THETA ** (-(jnp.arange(half, dtype=jnp.float32) * 2.0 / states.shape[-1]))
    angle = position.astype(jnp.float32)[:, None] * freq[None, :]
    cosine = jnp.cos(angle)
    sine = jnp.sin(angle)
    first = states[..., :half]
    second = states[..., half:]
    return jnp.concatenate(
        [first * cosine - second * sine, second * cosine + first * sine], axis=-1
    )


def group_of(slots, ends):
    return jnp.sum((ends[None, :] <= slots[:, None]).astype(jnp.int32), axis=1)


def butterfly_sum(x, axis, n):
    step = 1
    while step < n:
        x = x + lax.ppermute(x, axis, [(i, i ^ step) for i in range(n)])
        step *= 2
    return x


def halving_scatter(x, axis, n):
    rows = x.shape[0]
    me = lax.axis_index(axis)
    buf = x.reshape(rows, n, x.shape[1] // n)
    step = n // 2
    while step >= 1:
        half = buf.shape[1] // 2
        upper = (me // step) % 2
        keep = lax.dynamic_slice_in_dim(buf, upper * half, half, axis=1)
        send = lax.dynamic_slice_in_dim(buf, (1 - upper) * half, half, axis=1)
        buf = keep + lax.ppermute(send, axis, [(i, i ^ step) for i in range(n)])
        step //= 2
    return buf.reshape(rows, -1)


def doubling_gather(x, axis, n, order):
    me = lax.axis_index(axis)
    buf = x
    for step in order:
        other = lax.ppermute(buf, axis, [(i, i ^ step) for i in range(n)])
        upper = (me // step) % 2
        lo = jnp.where(upper == 0, buf, other)
        hi = jnp.where(upper == 0, other, buf)
        buf = jnp.concatenate([lo, hi], axis=0)
    bits = [step.bit_length() - 1 for step in order]
    rest = x.shape
    buf = buf.reshape((2,) * len(order) + rest)
    lead = [len(order) - 1 - s for s in range(len(order))]
    by_bit = sorted(range(len(order)), key=lambda s: -bits[s])
    buf = buf.transpose([lead[s] for s in by_bit] + list(range(len(order), len(order) + len(rest))))
    return buf.reshape((n * rest[0],) + rest[1:])


def partial_kernel(q_ref, qg_ref, qs_ref, pg_ref, k_ref, kg_ref, ks_ref, vt_ref, o_ref, *, scale, page):
    scores = lax.dot_general(
        k_ref[...], q_ref[...], (((1,), (1,)), ((), ())), preferred_element_type=jnp.float32
    ) * scale
    q_group = qg_ref[...]
    pages = pg_ref.shape[0]
    parts = [
        jnp.where(q_group == pg_ref[p], scores[p * page : (p + 1) * page], NEG) for p in range(pages)
    ]
    allowed = (kg_ref[...] == q_group) & (ks_ref[...] <= qs_ref[...])
    parts.append(jnp.where(allowed, scores[pages * page :], NEG))
    scores = jnp.concatenate(parts, axis=0)
    top = jnp.max(scores, axis=0, keepdims=True)
    top_hi = top.astype(jnp.bfloat16).astype(jnp.float32)
    top_lo = (top - top_hi).astype(jnp.bfloat16).astype(jnp.float32)
    base = jnp.where(top > 0.5 * NEG, top_hi + top_lo, 0.0)
    weights = jnp.exp(scores - base)
    total = jnp.sum(weights, axis=0, keepdims=True)
    total_hi = total.astype(jnp.bfloat16).astype(jnp.float32)
    total_lo = (total - total_hi).astype(jnp.bfloat16).astype(jnp.float32)
    numer = jnp.dot(vt_ref[...], weights.astype(jnp.bfloat16), preferred_element_type=jnp.float32)
    width = o_ref.shape[2]
    hd = vt_ref.shape[0]
    extra = o_ref.shape[1] - hd
    row = lax.broadcasted_iota(jnp.int32, (extra, top.shape[1]), 0)
    stats = jnp.where(
        row == 0, top_hi, jnp.where(row == 1, top_lo, jnp.where(row == 2, total_hi, jnp.where(row == 3, total_lo, 0.0)))
    )
    for j in range(o_ref.shape[0]):
        cols = slice(j * width, (j + 1) * width)
        o_ref[j, :hd, :] = numer[:, cols].astype(o_ref.dtype)
        o_ref[j, hd:, :] = stats[:, cols].astype(o_ref.dtype)


def local_partials(
    queries, q_group, q_slot, page_group, keys, k_group, k_slot, values_t, scale, owner_rows, block=512
):
    count, hd = queries.shape
    nk = keys.shape[0]
    tail = k_group.shape[0]
    page = (nk - tail) // page_group.shape[0]
    per = block // owner_rows
    return pl.pallas_call(
        functools.partial(partial_kernel, scale=scale, page=page),
        grid=(count // block,),
        in_specs=[
            pl.BlockSpec((block, hd), lambda i: (i, 0)),
            pl.BlockSpec((1, block), lambda i: (0, i)),
            pl.BlockSpec((1, block), lambda i: (0, i)),
            pl.BlockSpec(memory_space=pltpu.SMEM),
            pl.BlockSpec((nk, hd), lambda i: (0, 0)),
            pl.BlockSpec((tail, 1), lambda i: (0, 0)),
            pl.BlockSpec((tail, 1), lambda i: (0, 0)),
            pl.BlockSpec((hd, nk), lambda i: (0, 0)),
        ],
        out_specs=pl.BlockSpec((per, hd + 16, owner_rows), lambda i: (i, 0, 0)),
        out_shape=jax.ShapeDtypeStruct((count // owner_rows, hd + 16, owner_rows), jnp.bfloat16),
        cost_estimate=pl.CostEstimate(
            flops=4 * count * nk * hd, transcendentals=count * nk,
            bytes_accessed=2 * count * hd + 4 * nk * hd + 2 * count * (hd + 16),
        ),
    )(queries, q_group[None, :], q_slot[None, :], page_group, keys, k_group[:, None], k_slot[:, None], values_t)


def per_device(
    hidden,
    qkv_weight,
    q_gain,
    k_gain,
    key_cache,
    value_cache,
    page_table,
    suffix_lengths,
    token_slot,
    o_weight,
    norm_gain,
):
    tok_here = hidden.shape[0]
    local_width = q_gain.shape[0]
    group_count = suffix_lengths.shape[0]
    page_size = key_cache.shape[1]
    slots_here = key_cache.shape[0]
    page_total = page_table.shape[0]
    prefix_len = page_total * page_size // group_count
    scale = 1.0 / math.sqrt(HD)
    column = lax.axis_index("col")

    rows_n = D // local_width
    cols_n = page_total // slots_here
    row_order = [4, 2, 1, 8] if rows_n == 16 else [1 << i for i in range(rows_n.bit_length() - 1)]
    col_order = [4, 2, 16, 8, 1] if cols_n == 32 else [1 << i for i in range(cols_n.bit_length() - 1)]
    hidden_t = doubling_gather(hidden.T, "row", rows_n, row_order)
    weight_all = doubling_gather(qkv_weight, "col", cols_n, col_order)
    out_rows = doubling_gather(o_weight, "row", rows_n, row_order)
    out_weight_t = lax.all_gather(out_rows.T, "col", axis=0, tiled=True)

    projected = jnp.einsum(
        "dt,dcf->tcf", hidden_t, weight_all, preferred_element_type=jnp.float32
    )
    query_raw = projected[:, 0]
    key_raw = projected[:, 1]
    value_raw = projected[:, 2]
    squares = butterfly_sum(
        jnp.stack([jnp.sum(query_raw * query_raw, axis=1), jnp.sum(key_raw * key_raw, axis=1)]),
        "row",
        rows_n,
    )
    query_norm = query_raw * lax.rsqrt(squares[0] / D + EPS)[:, None] * q_gain
    key_norm = key_raw * lax.rsqrt(squares[1] / D + EPS)[:, None] * k_gain
    ends = jnp.cumsum(suffix_lengths)
    starts = ends - suffix_lengths
    my_slot = lax.dynamic_slice_in_dim(token_slot, column * tok_here, tok_here)
    my_group = group_of(my_slot, ends)
    begin = jnp.sum(
        jnp.where(
            my_group[:, None] == jnp.arange(group_count, dtype=jnp.int32)[None, :],
            starts[None, :],
            0,
        ),
        axis=1,
    )
    position = prefix_len + my_slot - begin
    query_rot = rotate(query_norm, position).astype(jnp.bfloat16)
    key_rot = rotate(key_norm, position).astype(jnp.bfloat16)
    value_here = value_raw.astype(jnp.bfloat16)

    all_query = doubling_gather(query_rot, "col", cols_n, col_order)
    their_group = group_of(token_slot, ends)

    page_slots = column * slots_here + jnp.arange(slots_here, dtype=jnp.int32)
    page_index = jnp.sum(
        jnp.where(
            page_table[None, :] == page_slots[:, None],
            jnp.arange(page_total, dtype=jnp.int32)[None, :],
            0,
        ),
        axis=1,
    )
    slot_group = page_index // (page_total // group_count)
    keys = jnp.concatenate([key_cache.reshape(slots_here * page_size, local_width), key_rot])
    values_t = jnp.concatenate(
        [value_cache.reshape(slots_here * page_size, local_width), value_here]
    ).T
    outgoing = local_partials(
        all_query, their_group, token_slot, slot_group, keys, my_group, my_slot, values_t, scale, tok_here
    )
    incoming = lax.all_to_all(outgoing, "col", split_axis=0, concat_axis=0, tiled=True)
    got_acc = incoming[:, :local_width, :].astype(jnp.float32)
    halves = incoming[:, local_width : local_width + 4, :].astype(jnp.float32)
    got_top = halves[:, 0] + halves[:, 1]
    got_sum = halves[:, 2] + halves[:, 3]
    biggest = jnp.max(got_top, axis=0)
    weight_owner = jnp.exp(got_top - biggest[None])
    denominator = jnp.sum(got_sum * weight_owner, axis=0)
    numerator = jnp.sum(got_acc * weight_owner[:, None, :], axis=0)
    attention_t = (numerator / denominator[None, :]).astype(jnp.bfloat16)
    heads_all = doubling_gather(attention_t, "row", rows_n, row_order)
    mixed = jnp.dot(heads_all.T, out_weight_t.T, preferred_element_type=jnp.float32)
    mean_sq = jnp.mean(mixed * mixed, axis=1)
    branch = lax.dynamic_slice_in_dim(mixed, lax.axis_index("row") * local_width, local_width, axis=1)
    result = hidden.astype(jnp.float32) + branch * lax.rsqrt(mean_sq + EPS)[:, None] * norm_gain
    return result


def solution(mesh):
    return jax.shard_map(
        per_device,
        mesh=mesh,
        in_specs=(
            P("col", "row"),
            P("col", None, "row"),
            P("row"),
            P("row"),
            P("col", None, "row"),
            P("col", None, "row"),
            P(),
            P(),
            P(),
            P("row", "col"),
            P("row"),
        ),
        out_specs=P("col", "row"),
        check_vma=False,
    )
```

```python
import math

import jax
import jax.numpy as jnp
import functools

from jax import lax
from jax.experimental import pallas as pl
from jax.experimental.pallas import tpu as pltpu
from jax.sharding import PartitionSpec as P

D = 2048
HD = 128


EPS = 1e-06
THETA = 500000.0
NEG = -1e30


def rotate(states, position):
    half = states.shape[-1] // 2
    freq = THETA ** (-(jnp.arange(half, dtype=jnp.float32) * 2.0 / states.shape[-1]))
    angle = position.astype(jnp.float32)[:, None] * freq[None, :]
    cosine = jnp.cos(angle)
    sine = jnp.sin(angle)
    first = states[..., :half]
    second = states[..., half:]
    return jnp.concatenate(
        [first * cosine - second * sine, second * cosine + first * sine], axis=-1
    )


def group_of(slots, ends):
    return jnp.sum((ends[None, :] <= slots[:, None]).astype(jnp.int32), axis=1)


def butterfly_sum(x, axis, n):
    step = 1
    while step < n:
        x = x + lax.ppermute(x, axis, [(i, i ^ step) for i in range(n)])
        step *= 2
    return x


def halving_scatter(x, axis, n):
    rows = x.shape[0]
    me = lax.axis_index(axis)
    buf = x.reshape(rows, n, x.shape[1] // n)
    step = n // 2
    while step >= 1:
        half = buf.shape[1] // 2
        upper = (me // step) % 2
        keep = lax.dynamic_slice_in_dim(buf, upper * half, half, axis=1)
        send = lax.dynamic_slice_in_dim(buf, (1 - upper) * half, half, axis=1)
        buf = keep + lax.ppermute(send, axis, [(i, i ^ step) for i in range(n)])
        step //= 2
    return buf.reshape(rows, -1)


def exchange_step(buf, axis, n, step):
    other = lax.ppermute(buf, axis, [(i, i ^ step) for i in range(n)])
    upper = (lax.axis_index(axis) // step) % 2
    lo = jnp.where(upper == 0, buf, other)
    hi = jnp.where(upper == 0, other, buf)
    return jnp.concatenate([lo, hi], axis=0)


def member_order(buf, n, order, rest):
    bits = [step.bit_length() - 1 for step in order]
    buf = buf.reshape((2,) * len(order) + rest)
    lead = [len(order) - 1 - s for s in range(len(order))]
    by_bit = sorted(range(len(order)), key=lambda s: -bits[s])
    buf = buf.transpose([lead[s] for s in by_bit] + list(range(len(order), len(order) + len(rest))))
    return buf.reshape((n * rest[0],) + rest[1:])


def doubling_gather(x, axis, n, order):
    buf = x
    for step in order:
        buf = exchange_step(buf, axis, n, step)
    return member_order(buf, n, order, x.shape)


def paired_gathers(first, first_axis, first_n, first_order, second, second_axis, second_n, second_order):
    a, b = first, second
    for k in range(max(len(first_order), len(second_order))):
        if k < len(first_order):
            a = exchange_step(a, first_axis, first_n, first_order[k])
        if k < len(second_order):
            b = exchange_step(b, second_axis, second_n, second_order[k])
        a, b = lax.optimization_barrier((a, b))
    return (
        member_order(a, first_n, first_order, first.shape),
        member_order(b, second_n, second_order, second.shape),
    )


def partial_kernel(q_ref, qg_ref, qs_ref, pg_ref, k_ref, kg_ref, ks_ref, vt_ref, o_ref, *, scale, page):
    scores = lax.dot_general(
        k_ref[...], q_ref[...], (((1,), (1,)), ((), ())), preferred_element_type=jnp.float32
    ) * scale
    q_group = qg_ref[...]
    pages = pg_ref.shape[0]
    parts = [
        jnp.where(q_group == pg_ref[p], scores[p * page : (p + 1) * page], NEG) for p in range(pages)
    ]
    allowed = (kg_ref[...] == q_group) & (ks_ref[...] <= qs_ref[...])
    parts.append(jnp.where(allowed, scores[pages * page :], NEG))
    scores = jnp.concatenate(parts, axis=0)
    top = jnp.max(scores, axis=0, keepdims=True)
    top_hi = top.astype(jnp.bfloat16).astype(jnp.float32)
    top_lo = (top - top_hi).astype(jnp.bfloat16).astype(jnp.float32)
    base = jnp.where(top > 0.5 * NEG, top_hi + top_lo, 0.0)
    weights = jnp.exp(scores - base)
    total = jnp.sum(weights, axis=0, keepdims=True)
    total_hi = total.astype(jnp.bfloat16).astype(jnp.float32)
    total_lo = (total - total_hi).astype(jnp.bfloat16).astype(jnp.float32)
    numer = jnp.dot(vt_ref[...], weights.astype(jnp.bfloat16), preferred_element_type=jnp.float32)
    width = o_ref.shape[2]
    hd = vt_ref.shape[0]
    extra = o_ref.shape[1] - hd
    row = lax.broadcasted_iota(jnp.int32, (extra, top.shape[1]), 0)
    stats = jnp.where(
        row == 0, top_hi, jnp.where(row == 1, top_lo, jnp.where(row == 2, total_hi, jnp.where(row == 3, total_lo, 0.0)))
    )
    for j in range(o_ref.shape[0]):
        cols = slice(j * width, (j + 1) * width)
        o_ref[j, :hd, :] = numer[:, cols].astype(o_ref.dtype)
        o_ref[j, hd:, :] = stats[:, cols].astype(o_ref.dtype)


def local_partials(
    queries, q_group, q_slot, page_group, keys, k_group, k_slot, values_t, scale, owner_rows, block=512
):
    count, hd = queries.shape
    nk = keys.shape[0]
    tail = k_group.shape[0]
    page = (nk - tail) // page_group.shape[0]
    per = block // owner_rows
    return pl.pallas_call(
        functools.partial(partial_kernel, scale=scale, page=page),
        grid=(count // block,),
        in_specs=[
            pl.BlockSpec((block, hd), lambda i: (i, 0)),
            pl.BlockSpec((1, block), lambda i: (0, i)),
            pl.BlockSpec((1, block), lambda i: (0, i)),
            pl.BlockSpec(memory_space=pltpu.SMEM),
            pl.BlockSpec((nk, hd), lambda i: (0, 0)),
            pl.BlockSpec((tail, 1), lambda i: (0, 0)),
            pl.BlockSpec((tail, 1), lambda i: (0, 0)),
            pl.BlockSpec((hd, nk), lambda i: (0, 0)),
        ],
        out_specs=pl.BlockSpec((per, hd + 16, owner_rows), lambda i: (i, 0, 0)),
        out_shape=jax.ShapeDtypeStruct((count // owner_rows, hd + 16, owner_rows), jnp.bfloat16),
        cost_estimate=pl.CostEstimate(
            flops=4 * count * nk * hd, transcendentals=count * nk,
            bytes_accessed=2 * count * hd + 4 * nk * hd + 2 * count * (hd + 16),
        ),
    )(queries, q_group[None, :], q_slot[None, :], page_group, keys, k_group[:, None], k_slot[:, None], values_t)


def per_device(
    hidden,
    qkv_weight,
    q_gain,
    k_gain,
    key_cache,
    value_cache,
    page_table,
    suffix_lengths,
    token_slot,
    o_weight,
    norm_gain,
):
    tok_here = hidden.shape[0]
    local_width = q_gain.shape[0]
    group_count = suffix_lengths.shape[0]
    page_size = key_cache.shape[1]
    slots_here = key_cache.shape[0]
    page_total = page_table.shape[0]
    prefix_len = page_total * page_size // group_count
    scale = 1.0 / math.sqrt(HD)
    column = lax.axis_index("col")

    rows_n = D // local_width
    cols_n = page_total // slots_here
    row_order = [4, 2, 1, 8] if rows_n == 16 else [1 << i for i in range(rows_n.bit_length() - 1)]
    col_order = [4, 2, 16, 8, 1] if cols_n == 32 else [1 << i for i in range(cols_n.bit_length() - 1)]
    row_parts, weight_all = paired_gathers(
        jnp.concatenate([hidden.T, o_weight], axis=1), "row", rows_n, row_order,
        qkv_weight, "col", cols_n, col_order,
    )
    hidden_t = row_parts[:, :tok_here]
    out_rows = row_parts[:, tok_here:]
    out_weight_t = lax.all_gather(out_rows.T, "col", axis=0, tiled=True)

    projected = jnp.einsum(
        "dt,dcf->tcf", hidden_t, weight_all, preferred_element_type=jnp.float32
    )
    query_raw = projected[:, 0]
    key_raw = projected[:, 1]
    value_raw = projected[:, 2]
    squares = butterfly_sum(
        jnp.stack([jnp.sum(query_raw * query_raw, axis=1), jnp.sum(key_raw * key_raw, axis=1)]),
        "row",
        rows_n,
    )
    query_norm = query_raw * lax.rsqrt(squares[0] / D + EPS)[:, None] * q_gain
    key_norm = key_raw * lax.rsqrt(squares[1] / D + EPS)[:, None] * k_gain
    ends = jnp.cumsum(suffix_lengths)
    starts = ends - suffix_lengths
    my_slot = lax.dynamic_slice_in_dim(token_slot, column * tok_here, tok_here)
    my_group = group_of(my_slot, ends)
    begin = jnp.sum(
        jnp.where(
            my_group[:, None] == jnp.arange(group_count, dtype=jnp.int32)[None, :],
            starts[None, :],
            0,
        ),
        axis=1,
    )
    position = prefix_len + my_slot - begin
    query_rot = rotate(query_norm, position).astype(jnp.bfloat16)
    key_rot = rotate(key_norm, position).astype(jnp.bfloat16)
    value_here = value_raw.astype(jnp.bfloat16)

    all_query = doubling_gather(query_rot, "col", cols_n, col_order)
    their_group = group_of(token_slot, ends)

    page_slots = column * slots_here + jnp.arange(slots_here, dtype=jnp.int32)
    page_index = jnp.sum(
        jnp.where(
            page_table[None, :] == page_slots[:, None],
            jnp.arange(page_total, dtype=jnp.int32)[None, :],
            0,
        ),
        axis=1,
    )
    slot_group = page_index // (page_total // group_count)
    keys = jnp.concatenate([key_cache.reshape(slots_here * page_size, local_width), key_rot])
    values_t = jnp.concatenate(
        [value_cache.reshape(slots_here * page_size, local_width), value_here]
    ).T
    outgoing = local_partials(
        all_query, their_group, token_slot, slot_group, keys, my_group, my_slot, values_t, scale, tok_here
    )
    incoming = lax.all_to_all(outgoing, "col", split_axis=0, concat_axis=0, tiled=True)
    got_acc = incoming[:, :local_width, :].astype(jnp.float32)
    halves = incoming[:, local_width : local_width + 4, :].astype(jnp.float32)
    got_top = halves[:, 0] + halves[:, 1]
    got_sum = halves[:, 2] + halves[:, 3]
    biggest = jnp.max(got_top, axis=0)
    weight_owner = jnp.exp(got_top - biggest[None])
    denominator = jnp.sum(got_sum * weight_owner, axis=0)
    numerator = jnp.sum(got_acc * weight_owner[:, None, :], axis=0)
    attention_t = (numerator / denominator[None, :]).astype(jnp.bfloat16)
    heads_all = doubling_gather(attention_t, "row", rows_n, row_order)
    mixed = jnp.dot(heads_all.T, out_weight_t.T, preferred_element_type=jnp.float32)
    mean_sq = jnp.mean(mixed * mixed, axis=1)
    branch = lax.dynamic_slice_in_dim(mixed, lax.axis_index("row") * local_width, local_width, axis=1)
    result = hidden.astype(jnp.float32) + branch * lax.rsqrt(mean_sq + EPS)[:, None] * norm_gain
    return result


def solution(mesh):
    return jax.shard_map(
        per_device,
        mesh=mesh,
        in_specs=(
            P("col", "row"),
            P("col", None, "row"),
            P("row"),
            P("row"),
            P("col", None, "row"),
            P("col", None, "row"),
            P(),
            P(),
            P(),
            P("row", "col"),
            P("row"),
        ),
        out_specs=P("col", "row"),
        check_vma=False,
    )
```

```python
import math

import jax
import jax.numpy as jnp
import functools

from jax import lax
from jax.experimental import pallas as pl
from jax.experimental.pallas import tpu as pltpu
from jax.sharding import PartitionSpec as P

D = 2048
HD = 128


EPS = 1e-06
THETA = 500000.0
NEG = -1e30


def rotate(states, position):
    half = states.shape[-1] // 2
    freq = THETA ** (-(jnp.arange(half, dtype=jnp.float32) * 2.0 / states.shape[-1]))
    angle = position.astype(jnp.float32)[:, None] * freq[None, :]
    cosine = jnp.cos(angle)
    sine = jnp.sin(angle)
    first = states[..., :half]
    second = states[..., half:]
    return jnp.concatenate(
        [first * cosine - second * sine, second * cosine + first * sine], axis=-1
    )


def group_of(slots, ends):
    return jnp.sum((ends[None, :] <= slots[:, None]).astype(jnp.int32), axis=1)


def butterfly_sum(x, axis, n):
    step = 1
    while step < n:
        x = x + lax.ppermute(x, axis, [(i, i ^ step) for i in range(n)])
        step *= 2
    return x


def halving_scatter(x, axis, n):
    rows = x.shape[0]
    me = lax.axis_index(axis)
    buf = x.reshape(rows, n, x.shape[1] // n)
    step = n // 2
    while step >= 1:
        half = buf.shape[1] // 2
        upper = (me // step) % 2
        keep = lax.dynamic_slice_in_dim(buf, upper * half, half, axis=1)
        send = lax.dynamic_slice_in_dim(buf, (1 - upper) * half, half, axis=1)
        buf = keep + lax.ppermute(send, axis, [(i, i ^ step) for i in range(n)])
        step //= 2
    return buf.reshape(rows, -1)


def exchange_step(buf, axis, n, step):
    other = lax.ppermute(buf, axis, [(i, i ^ step) for i in range(n)])
    upper = (lax.axis_index(axis) // step) % 2
    size = buf.shape[0]
    both = jnp.zeros((2 * size,) + buf.shape[1:], buf.dtype)
    both = lax.dynamic_update_slice_in_dim(both, buf, upper * size, axis=0)
    return lax.dynamic_update_slice_in_dim(both, other, (1 - upper) * size, axis=0)


def member_order(buf, n, order, rest):
    bits = [step.bit_length() - 1 for step in order]
    buf = buf.reshape((2,) * len(order) + rest)
    lead = [len(order) - 1 - s for s in range(len(order))]
    by_bit = sorted(range(len(order)), key=lambda s: -bits[s])
    buf = buf.transpose([lead[s] for s in by_bit] + list(range(len(order), len(order) + len(rest))))
    return buf.reshape((n * rest[0],) + rest[1:])


def doubling_gather(x, axis, n, order):
    buf = x
    for step in order:
        buf = exchange_step(buf, axis, n, step)
    return member_order(buf, n, order, x.shape)


def paired_gathers(first, first_axis, first_n, first_order, second, second_axis, second_n, second_order):
    a, b = first, second
    for k in range(max(len(first_order), len(second_order))):
        if k < len(first_order):
            a = exchange_step(a, first_axis, first_n, first_order[k])
        if k < len(second_order):
            b = exchange_step(b, second_axis, second_n, second_order[k])
        a, b = lax.optimization_barrier((a, b))
    return (
        member_order(a, first_n, first_order, first.shape),
        member_order(b, second_n, second_order, second.shape),
    )


def partial_kernel(q_ref, qg_ref, qs_ref, pg_ref, k_ref, kg_ref, ks_ref, vt_ref, o_ref, *, scale, page):
    scores = lax.dot_general(
        k_ref[...], q_ref[...], (((1,), (1,)), ((), ())), preferred_element_type=jnp.float32
    ) * scale
    q_group = qg_ref[...]
    pages = pg_ref.shape[0]
    parts = [
        jnp.where(q_group == pg_ref[p], scores[p * page : (p + 1) * page], NEG) for p in range(pages)
    ]
    allowed = (kg_ref[...] == q_group) & (ks_ref[...] <= qs_ref[...])
    parts.append(jnp.where(allowed, scores[pages * page :], NEG))
    scores = jnp.concatenate(parts, axis=0)
    top = jnp.max(scores, axis=0, keepdims=True)
    top_hi = top.astype(jnp.bfloat16).astype(jnp.float32)
    top_lo = (top - top_hi).astype(jnp.bfloat16).astype(jnp.float32)
    base = jnp.where(top > 0.5 * NEG, top_hi + top_lo, 0.0)
    weights = jnp.exp(scores - base)
    total = jnp.sum(weights, axis=0, keepdims=True)
    total_hi = total.astype(jnp.bfloat16).astype(jnp.float32)
    total_lo = (total - total_hi).astype(jnp.bfloat16).astype(jnp.float32)
    numer = jnp.dot(vt_ref[...], weights.astype(jnp.bfloat16), preferred_element_type=jnp.float32)
    width = o_ref.shape[2]
    hd = vt_ref.shape[0]
    extra = o_ref.shape[1] - hd
    row = lax.broadcasted_iota(jnp.int32, (extra, top.shape[1]), 0)
    stats = jnp.where(
        row == 0, top_hi, jnp.where(row == 1, top_lo, jnp.where(row == 2, total_hi, jnp.where(row == 3, total_lo, 0.0)))
    )
    for j in range(o_ref.shape[0]):
        cols = slice(j * width, (j + 1) * width)
        o_ref[j, :hd, :] = numer[:, cols].astype(o_ref.dtype)
        o_ref[j, hd:, :] = stats[:, cols].astype(o_ref.dtype)


def local_partials(
    queries, q_group, q_slot, page_group, keys, k_group, k_slot, values_t, scale, owner_rows, block=512
):
    count, hd = queries.shape
    nk = keys.shape[0]
    tail = k_group.shape[0]
    page = (nk - tail) // page_group.shape[0]
    per = block // owner_rows
    return pl.pallas_call(
        functools.partial(partial_kernel, scale=scale, page=page),
        grid=(count // block,),
        in_specs=[
            pl.BlockSpec((block, hd), lambda i: (i, 0)),
            pl.BlockSpec((1, block), lambda i: (0, i)),
            pl.BlockSpec((1, block), lambda i: (0, i)),
            pl.BlockSpec(memory_space=pltpu.SMEM),
            pl.BlockSpec((nk, hd), lambda i: (0, 0)),
            pl.BlockSpec((tail, 1), lambda i: (0, 0)),
            pl.BlockSpec((tail, 1), lambda i: (0, 0)),
            pl.BlockSpec((hd, nk), lambda i: (0, 0)),
        ],
        out_specs=pl.BlockSpec((per, hd + 16, owner_rows), lambda i: (i, 0, 0)),
        out_shape=jax.ShapeDtypeStruct((count // owner_rows, hd + 16, owner_rows), jnp.bfloat16),
        cost_estimate=pl.CostEstimate(
            flops=4 * count * nk * hd, transcendentals=count * nk,
            bytes_accessed=2 * count * hd + 4 * nk * hd + 2 * count * (hd + 16),
        ),
    )(queries, q_group[None, :], q_slot[None, :], page_group, keys, k_group[:, None], k_slot[:, None], values_t)


def per_device(
    hidden,
    qkv_weight,
    q_gain,
    k_gain,
    key_cache,
    value_cache,
    page_table,
    suffix_lengths,
    token_slot,
    o_weight,
    norm_gain,
):
    tok_here = hidden.shape[0]
    local_width = q_gain.shape[0]
    group_count = suffix_lengths.shape[0]
    page_size = key_cache.shape[1]
    slots_here = key_cache.shape[0]
    page_total = page_table.shape[0]
    prefix_len = page_total * page_size // group_count
    scale = 1.0 / math.sqrt(HD)
    column = lax.axis_index("col")

    rows_n = D // local_width
    cols_n = page_total // slots_here
    row_order = [4, 2, 1, 8] if rows_n == 16 else [1 << i for i in range(rows_n.bit_length() - 1)]
    col_order = [4, 2, 16, 8, 1] if cols_n == 32 else [1 << i for i in range(cols_n.bit_length() - 1)]
    row_parts, weight_all = paired_gathers(
        jnp.concatenate([hidden.T, o_weight], axis=1), "row", rows_n, row_order,
        qkv_weight, "col", cols_n, col_order,
    )
    hidden_t = row_parts[:, :tok_here]
    out_rows = row_parts[:, tok_here:]
    out_weight_t = lax.all_gather(out_rows.T, "col", axis=0, tiled=True)

    projected = jnp.einsum(
        "dt,dcf->tcf", hidden_t, weight_all, preferred_element_type=jnp.float32
    )
    query_raw = projected[:, 0]
    key_raw = projected[:, 1]
    value_raw = projected[:, 2]
    squares = butterfly_sum(
        jnp.stack([jnp.sum(query_raw * query_raw, axis=1), jnp.sum(key_raw * key_raw, axis=1)]),
        "row",
        rows_n,
    )
    query_norm = query_raw * lax.rsqrt(squares[0] / D + EPS)[:, None] * q_gain
    key_norm = key_raw * lax.rsqrt(squares[1] / D + EPS)[:, None] * k_gain
    ends = jnp.cumsum(suffix_lengths)
    starts = ends - suffix_lengths
    my_slot = lax.dynamic_slice_in_dim(token_slot, column * tok_here, tok_here)
    my_group = group_of(my_slot, ends)
    begin = jnp.sum(
        jnp.where(
            my_group[:, None] == jnp.arange(group_count, dtype=jnp.int32)[None, :],
            starts[None, :],
            0,
        ),
        axis=1,
    )
    position = prefix_len + my_slot - begin
    query_rot = rotate(query_norm, position).astype(jnp.bfloat16)
    key_rot = rotate(key_norm, position).astype(jnp.bfloat16)
    value_here = value_raw.astype(jnp.bfloat16)

    all_query = doubling_gather(query_rot, "col", cols_n, col_order)
    their_group = group_of(token_slot, ends)

    page_slots = column * slots_here + jnp.arange(slots_here, dtype=jnp.int32)
    page_index = jnp.sum(
        jnp.where(
            page_table[None, :] == page_slots[:, None],
            jnp.arange(page_total, dtype=jnp.int32)[None, :],
            0,
        ),
        axis=1,
    )
    slot_group = page_index // (page_total // group_count)
    keys = jnp.concatenate([key_cache.reshape(slots_here * page_size, local_width), key_rot])
    values_t = jnp.concatenate(
        [value_cache.reshape(slots_here * page_size, local_width), value_here]
    ).T
    outgoing = local_partials(
        all_query, their_group, token_slot, slot_group, keys, my_group, my_slot, values_t, scale, tok_here
    )
    incoming = lax.all_to_all(outgoing, "col", split_axis=0, concat_axis=0, tiled=True)
    got_acc = incoming[:, :local_width, :].astype(jnp.float32)
    halves = incoming[:, local_width : local_width + 4, :].astype(jnp.float32)
    got_top = halves[:, 0] + halves[:, 1]
    got_sum = halves[:, 2] + halves[:, 3]
    biggest = jnp.max(got_top, axis=0)
    weight_owner = jnp.exp(got_top - biggest[None])
    denominator = jnp.sum(got_sum * weight_owner, axis=0)
    numerator = jnp.sum(got_acc * weight_owner[:, None, :], axis=0)
    attention_t = (numerator / denominator[None, :]).astype(jnp.bfloat16)
    heads_all = doubling_gather(attention_t, "row", rows_n, row_order)
    mixed = jnp.dot(heads_all.T, out_weight_t.T, preferred_element_type=jnp.float32)
    mean_sq = jnp.mean(mixed * mixed, axis=1)
    branch = lax.dynamic_slice_in_dim(mixed, lax.axis_index("row") * local_width, local_width, axis=1)
    result = hidden.astype(jnp.float32) + branch * lax.rsqrt(mean_sq + EPS)[:, None] * norm_gain
    return result


def solution(mesh):
    return jax.shard_map(
        per_device,
        mesh=mesh,
        in_specs=(
            P("col", "row"),
            P("col", None, "row"),
            P("row"),
            P("row"),
            P("col", None, "row"),
            P("col", None, "row"),
            P(),
            P(),
            P(),
            P("row", "col"),
            P("row"),
        ),
        out_specs=P("col", "row"),
        check_vma=False,
    )
```

```python
import math

import jax
import jax.numpy as jnp
import functools

from jax import lax
from jax.experimental import pallas as pl
from jax.experimental.pallas import tpu as pltpu
from jax.sharding import PartitionSpec as P

D = 2048
HD = 128


EPS = 1e-06
THETA = 500000.0
NEG = -1e30


def rotate(states, position):
    half = states.shape[-1] // 2
    freq = THETA ** (-(jnp.arange(half, dtype=jnp.float32) * 2.0 / states.shape[-1]))
    angle = position.astype(jnp.float32)[:, None] * freq[None, :]
    cosine = jnp.cos(angle)
    sine = jnp.sin(angle)
    first = states[..., :half]
    second = states[..., half:]
    return jnp.concatenate(
        [first * cosine - second * sine, second * cosine + first * sine], axis=-1
    )


def group_of(slots, ends):
    return jnp.sum((ends[None, :] <= slots[:, None]).astype(jnp.int32), axis=1)


def butterfly_sum(x, axis, n):
    step = 1
    while step < n:
        x = x + lax.ppermute(x, axis, [(i, i ^ step) for i in range(n)])
        step *= 2
    return x


def halving_scatter(x, axis, n):
    rows = x.shape[0]
    me = lax.axis_index(axis)
    buf = x.reshape(rows, n, x.shape[1] // n)
    step = n // 2
    while step >= 1:
        half = buf.shape[1] // 2
        upper = (me // step) % 2
        keep = lax.dynamic_slice_in_dim(buf, upper * half, half, axis=1)
        send = lax.dynamic_slice_in_dim(buf, (1 - upper) * half, half, axis=1)
        buf = keep + lax.ppermute(send, axis, [(i, i ^ step) for i in range(n)])
        step //= 2
    return buf.reshape(rows, -1)


def exchange_step(buf, axis, n, step):
    other = lax.ppermute(buf, axis, [(i, i ^ step) for i in range(n)])
    upper = (lax.axis_index(axis) // step) % 2
    size = buf.shape[0]
    both = jnp.zeros((2 * size,) + buf.shape[1:], buf.dtype)
    both = lax.dynamic_update_slice_in_dim(both, buf, upper * size, axis=0)
    return lax.dynamic_update_slice_in_dim(both, other, (1 - upper) * size, axis=0)


def member_order(buf, n, order, rest):
    bits = [step.bit_length() - 1 for step in order]
    buf = buf.reshape((2,) * len(order) + rest)
    lead = [len(order) - 1 - s for s in range(len(order))]
    by_bit = sorted(range(len(order)), key=lambda s: -bits[s])
    buf = buf.transpose([lead[s] for s in by_bit] + list(range(len(order), len(order) + len(rest))))
    return buf.reshape((n * rest[0],) + rest[1:])


def doubling_gather(x, axis, n, order):
    buf = x
    for step in order:
        buf = exchange_step(buf, axis, n, step)
    return member_order(buf, n, order, x.shape)


def paired_gathers(first, first_axis, first_n, first_order, second, second_axis, second_n, second_order):
    a, b = first, second
    for k in range(max(len(first_order), len(second_order))):
        if k < len(first_order):
            a = exchange_step(a, first_axis, first_n, first_order[k])
        if k < len(second_order):
            b = exchange_step(b, second_axis, second_n, second_order[k])
        a, b = lax.optimization_barrier((a, b))
    return (
        member_order(a, first_n, first_order, first.shape),
        member_order(b, second_n, second_order, second.shape),
    )


def partial_kernel(q_ref, qg_ref, qs_ref, pg_ref, k_ref, kg_ref, ks_ref, vt_ref, o_ref, *, scale, page):
    scores = lax.dot_general(
        k_ref[...], q_ref[...], (((1,), (1,)), ((), ())), preferred_element_type=jnp.float32
    ) * scale
    q_group = qg_ref[...]
    pages = pg_ref.shape[0]
    parts = [
        jnp.where(q_group == pg_ref[p], scores[p * page : (p + 1) * page], NEG) for p in range(pages)
    ]
    allowed = (kg_ref[...] == q_group) & (ks_ref[...] <= qs_ref[...])
    parts.append(jnp.where(allowed, scores[pages * page :], NEG))
    scores = jnp.concatenate(parts, axis=0)
    top = jnp.max(scores, axis=0, keepdims=True)
    top_hi = top.astype(jnp.bfloat16).astype(jnp.float32)
    top_lo = (top - top_hi).astype(jnp.bfloat16).astype(jnp.float32)
    base = jnp.where(top > 0.5 * NEG, top_hi + top_lo, 0.0)
    weights = jnp.exp(scores - base)
    total = jnp.sum(weights, axis=0, keepdims=True)
    total_hi = total.astype(jnp.bfloat16).astype(jnp.float32)
    total_lo = (total - total_hi).astype(jnp.bfloat16).astype(jnp.float32)
    numer = jnp.dot(vt_ref[...], weights.astype(jnp.bfloat16), preferred_element_type=jnp.float32)
    width = o_ref.shape[2]
    hd = vt_ref.shape[0]
    extra = o_ref.shape[1] - hd
    row = lax.broadcasted_iota(jnp.int32, (extra, top.shape[1]), 0)
    stats = jnp.where(
        row == 0, top_hi, jnp.where(row == 1, top_lo, jnp.where(row == 2, total_hi, jnp.where(row == 3, total_lo, 0.0)))
    )
    for j in range(o_ref.shape[0]):
        cols = slice(j * width, (j + 1) * width)
        o_ref[j, :hd, :] = numer[:, cols].astype(o_ref.dtype)
        o_ref[j, hd:, :] = stats[:, cols].astype(o_ref.dtype)


def local_partials(
    queries, q_group, q_slot, page_group, keys, k_group, k_slot, values_t, scale, owner_rows, block=512
):
    count, hd = queries.shape
    nk = keys.shape[0]
    tail = k_group.shape[0]
    page = (nk - tail) // page_group.shape[0]
    per = block // owner_rows
    return pl.pallas_call(
        functools.partial(partial_kernel, scale=scale, page=page),
        grid=(count // block,),
        in_specs=[
            pl.BlockSpec((block, hd), lambda i: (i, 0)),
            pl.BlockSpec((1, block), lambda i: (0, i)),
            pl.BlockSpec((1, block), lambda i: (0, i)),
            pl.BlockSpec(memory_space=pltpu.SMEM),
            pl.BlockSpec((nk, hd), lambda i: (0, 0)),
            pl.BlockSpec((tail, 1), lambda i: (0, 0)),
            pl.BlockSpec((tail, 1), lambda i: (0, 0)),
            pl.BlockSpec((hd, nk), lambda i: (0, 0)),
        ],
        out_specs=pl.BlockSpec((per, hd + 4, owner_rows), lambda i: (i, 0, 0)),
        out_shape=jax.ShapeDtypeStruct((count // owner_rows, hd + 4, owner_rows), jnp.bfloat16),
        cost_estimate=pl.CostEstimate(
            flops=4 * count * nk * hd, transcendentals=count * nk,
            bytes_accessed=2 * count * hd + 4 * nk * hd + 2 * count * (hd + 4),
        ),
    )(queries, q_group[None, :], q_slot[None, :], page_group, keys, k_group[:, None], k_slot[:, None], values_t)


def per_device(
    hidden,
    qkv_weight,
    q_gain,
    k_gain,
    key_cache,
    value_cache,
    page_table,
    suffix_lengths,
    token_slot,
    o_weight,
    norm_gain,
):
    tok_here = hidden.shape[0]
    local_width = q_gain.shape[0]
    group_count = suffix_lengths.shape[0]
    page_size = key_cache.shape[1]
    slots_here = key_cache.shape[0]
    page_total = page_table.shape[0]
    prefix_len = page_total * page_size // group_count
    scale = 1.0 / math.sqrt(HD)
    column = lax.axis_index("col")

    rows_n = D // local_width
    cols_n = page_total // slots_here
    row_order = [4, 2, 1, 8] if rows_n == 16 else [1 << i for i in range(rows_n.bit_length() - 1)]
    col_order = [4, 2, 16, 8, 1] if cols_n == 32 else [1 << i for i in range(cols_n.bit_length() - 1)]
    row_parts, weight_all = paired_gathers(
        jnp.concatenate([hidden.T, o_weight], axis=1), "row", rows_n, row_order,
        qkv_weight, "col", cols_n, col_order,
    )
    hidden_t = row_parts[:, :tok_here]
    out_rows = row_parts[:, tok_here:]
    out_weight_t = lax.all_gather(out_rows.T, "col", axis=0, tiled=True)

    projected = jnp.einsum(
        "dt,dcf->tcf", hidden_t, weight_all, preferred_element_type=jnp.float32
    )
    query_raw = projected[:, 0]
    key_raw = projected[:, 1]
    value_raw = projected[:, 2]
    squares = butterfly_sum(
        jnp.stack([jnp.sum(query_raw * query_raw, axis=1), jnp.sum(key_raw * key_raw, axis=1)]),
        "row",
        rows_n,
    )
    query_norm = query_raw * lax.rsqrt(squares[0] / D + EPS)[:, None] * q_gain
    key_norm = key_raw * lax.rsqrt(squares[1] / D + EPS)[:, None] * k_gain
    ends = jnp.cumsum(suffix_lengths)
    starts = ends - suffix_lengths
    my_slot = lax.dynamic_slice_in_dim(token_slot, column * tok_here, tok_here)
    my_group = group_of(my_slot, ends)
    begin = jnp.sum(
        jnp.where(
            my_group[:, None] == jnp.arange(group_count, dtype=jnp.int32)[None, :],
            starts[None, :],
            0,
        ),
        axis=1,
    )
    position = prefix_len + my_slot - begin
    query_rot = rotate(query_norm, position).astype(jnp.bfloat16)
    key_rot = rotate(key_norm, position).astype(jnp.bfloat16)
    value_here = value_raw.astype(jnp.bfloat16)

    all_query = doubling_gather(query_rot, "col", cols_n, col_order)
    their_group = group_of(token_slot, ends)

    page_slots = column * slots_here + jnp.arange(slots_here, dtype=jnp.int32)
    page_index = jnp.sum(
        jnp.where(
            page_table[None, :] == page_slots[:, None],
            jnp.arange(page_total, dtype=jnp.int32)[None, :],
            0,
        ),
        axis=1,
    )
    slot_group = page_index // (page_total // group_count)
    keys = jnp.concatenate([key_cache.reshape(slots_here * page_size, local_width), key_rot])
    values_t = jnp.concatenate(
        [value_cache.reshape(slots_here * page_size, local_width), value_here]
    ).T
    outgoing = local_partials(
        all_query, their_group, token_slot, slot_group, keys, my_group, my_slot, values_t, scale, tok_here
    )
    incoming = lax.all_to_all(outgoing, "col", split_axis=0, concat_axis=0, tiled=True)
    got_acc = incoming[:, :local_width, :].astype(jnp.float32)
    halves = incoming[:, local_width : local_width + 4, :].astype(jnp.float32)
    got_top = halves[:, 0] + halves[:, 1]
    got_sum = halves[:, 2] + halves[:, 3]
    biggest = jnp.max(got_top, axis=0)
    weight_owner = jnp.exp(got_top - biggest[None])
    denominator = jnp.sum(got_sum * weight_owner, axis=0)
    numerator = jnp.sum(got_acc * weight_owner[:, None, :], axis=0)
    attention_t = (numerator / denominator[None, :]).astype(jnp.bfloat16)
    heads_all = doubling_gather(attention_t, "row", rows_n, row_order)
    mixed = jnp.dot(heads_all.T, out_weight_t.T, preferred_element_type=jnp.float32)
    mean_sq = jnp.mean(mixed * mixed, axis=1)
    branch = lax.dynamic_slice_in_dim(mixed, lax.axis_index("row") * local_width, local_width, axis=1)
    result = hidden.astype(jnp.float32) + branch * lax.rsqrt(mean_sq + EPS)[:, None] * norm_gain
    return result


def solution(mesh):
    return jax.shard_map(
        per_device,
        mesh=mesh,
        in_specs=(
            P("col", "row"),
            P("col", None, "row"),
            P("row"),
            P("row"),
            P("col", None, "row"),
            P("col", None, "row"),
            P(),
            P(),
            P(),
            P("row", "col"),
            P("row"),
        ),
        out_specs=P("col", "row"),
        check_vma=False,
    )
```

```python
import math

import jax
import jax.numpy as jnp
import functools

from jax import lax
from jax.experimental import pallas as pl
from jax.experimental.pallas import tpu as pltpu
from jax.sharding import PartitionSpec as P

D = 2048
HD = 128


EPS = 1e-06
THETA = 500000.0
NEG = -1e30


def rotate(states, position):
    half = states.shape[-1] // 2
    freq = THETA ** (-(jnp.arange(half, dtype=jnp.float32) * 2.0 / states.shape[-1]))
    angle = position.astype(jnp.float32)[:, None] * freq[None, :]
    cosine = jnp.cos(angle)
    sine = jnp.sin(angle)
    first = states[..., :half]
    second = states[..., half:]
    return jnp.concatenate(
        [first * cosine - second * sine, second * cosine + first * sine], axis=-1
    )


def group_of(slots, ends):
    return jnp.sum((ends[None, :] <= slots[:, None]).astype(jnp.int32), axis=1)


def butterfly_sum(x, axis, n):
    step = 1
    while step < n:
        x = x + lax.ppermute(x, axis, [(i, i ^ step) for i in range(n)])
        step *= 2
    return x


def halving_scatter(x, axis, n):
    rows = x.shape[0]
    me = lax.axis_index(axis)
    buf = x.reshape(rows, n, x.shape[1] // n)
    step = n // 2
    while step >= 1:
        half = buf.shape[1] // 2
        upper = (me // step) % 2
        keep = lax.dynamic_slice_in_dim(buf, upper * half, half, axis=1)
        send = lax.dynamic_slice_in_dim(buf, (1 - upper) * half, half, axis=1)
        buf = keep + lax.ppermute(send, axis, [(i, i ^ step) for i in range(n)])
        step //= 2
    return buf.reshape(rows, -1)


def exchange_step(buf, axis, n, step):
    other = lax.ppermute(buf, axis, [(i, i ^ step) for i in range(n)])
    upper = (lax.axis_index(axis) // step) % 2
    size = buf.shape[0]
    both = jnp.zeros((2 * size,) + buf.shape[1:], buf.dtype)
    both = lax.dynamic_update_slice_in_dim(both, buf, upper * size, axis=0)
    return lax.dynamic_update_slice_in_dim(both, other, (1 - upper) * size, axis=0)


def member_order(buf, n, order, rest):
    bits = [step.bit_length() - 1 for step in order]
    buf = buf.reshape((2,) * len(order) + rest)
    lead = [len(order) - 1 - s for s in range(len(order))]
    by_bit = sorted(range(len(order)), key=lambda s: -bits[s])
    buf = buf.transpose([lead[s] for s in by_bit] + list(range(len(order), len(order) + len(rest))))
    return buf.reshape((n * rest[0],) + rest[1:])


def doubling_gather(x, axis, n, order):
    buf = x
    for step in order:
        buf = exchange_step(buf, axis, n, step)
    return member_order(buf, n, order, x.shape)


def paired_gathers(first, first_axis, first_n, first_order, second, second_axis, second_n, second_order):
    a, b = first, second
    for k in range(max(len(first_order), len(second_order))):
        if k < len(first_order):
            a = exchange_step(a, first_axis, first_n, first_order[k])
        if k < len(second_order):
            b = exchange_step(b, second_axis, second_n, second_order[k])
        a, b = lax.optimization_barrier((a, b))
    return (
        member_order(a, first_n, first_order, first.shape),
        member_order(b, second_n, second_order, second.shape),
    )


def partial_kernel(q_ref, qg_ref, qs_ref, pg_ref, k_ref, kg_ref, ks_ref, vt_ref, o_ref, *, scale, page):
    scores = lax.dot_general(
        k_ref[...], q_ref[...], (((1,), (1,)), ((), ())), preferred_element_type=jnp.float32
    ) * scale
    q_group = qg_ref[...]
    pages = pg_ref.shape[0]
    parts = [
        jnp.where(q_group == pg_ref[p], scores[p * page : (p + 1) * page], NEG) for p in range(pages)
    ]
    allowed = (kg_ref[...] == q_group) & (ks_ref[...] <= qs_ref[...])
    parts.append(jnp.where(allowed, scores[pages * page :], NEG))
    scores = jnp.concatenate(parts, axis=0)
    top = jnp.max(scores, axis=0, keepdims=True)
    top_hi = top.astype(jnp.bfloat16).astype(jnp.float32)
    top_lo = (top - top_hi).astype(jnp.bfloat16).astype(jnp.float32)
    base = jnp.where(top > 0.5 * NEG, top_hi + top_lo, 0.0)
    weights = jnp.exp(scores - base)
    total = jnp.sum(weights, axis=0, keepdims=True)
    total_hi = total.astype(jnp.bfloat16).astype(jnp.float32)
    total_lo = (total - total_hi).astype(jnp.bfloat16).astype(jnp.float32)
    numer = jnp.dot(vt_ref[...], weights.astype(jnp.bfloat16), preferred_element_type=jnp.float32)
    width = o_ref.shape[2]
    hd = vt_ref.shape[0]
    extra = o_ref.shape[1] - hd
    row = lax.broadcasted_iota(jnp.int32, (extra, top.shape[1]), 0)
    stats = jnp.where(
        row == 0, top_hi, jnp.where(row == 1, top_lo, jnp.where(row == 2, total_hi, jnp.where(row == 3, total_lo, 0.0)))
    )
    for j in range(o_ref.shape[0]):
        cols = slice(j * width, (j + 1) * width)
        o_ref[j, :hd, :] = numer[:, cols].astype(o_ref.dtype)
        o_ref[j, hd:, :] = stats[:, cols].astype(o_ref.dtype)


def local_partials(
    queries, q_group, q_slot, page_group, keys, k_group, k_slot, values_t, scale, owner_rows, block=1024
):
    count, hd = queries.shape
    nk = keys.shape[0]
    tail = k_group.shape[0]
    page = (nk - tail) // page_group.shape[0]
    per = block // owner_rows
    return pl.pallas_call(
        functools.partial(partial_kernel, scale=scale, page=page),
        grid=(count // block,),
        in_specs=[
            pl.BlockSpec((block, hd), lambda i: (i, 0)),
            pl.BlockSpec((1, block), lambda i: (0, i)),
            pl.BlockSpec((1, block), lambda i: (0, i)),
            pl.BlockSpec(memory_space=pltpu.SMEM),
            pl.BlockSpec((nk, hd), lambda i: (0, 0)),
            pl.BlockSpec((tail, 1), lambda i: (0, 0)),
            pl.BlockSpec((tail, 1), lambda i: (0, 0)),
            pl.BlockSpec((hd, nk), lambda i: (0, 0)),
        ],
        out_specs=pl.BlockSpec((per, hd + 4, owner_rows), lambda i: (i, 0, 0)),
        out_shape=jax.ShapeDtypeStruct((count // owner_rows, hd + 4, owner_rows), jnp.bfloat16),
        cost_estimate=pl.CostEstimate(
            flops=4 * count * nk * hd, transcendentals=count * nk,
            bytes_accessed=2 * count * hd + 4 * nk * hd + 2 * count * (hd + 4),
        ),
    )(queries, q_group[None, :], q_slot[None, :], page_group, keys, k_group[:, None], k_slot[:, None], values_t)


def per_device(
    hidden,
    qkv_weight,
    q_gain,
    k_gain,
    key_cache,
    value_cache,
    page_table,
    suffix_lengths,
    token_slot,
    o_weight,
    norm_gain,
):
    tok_here = hidden.shape[0]
    local_width = q_gain.shape[0]
    group_count = suffix_lengths.shape[0]
    page_size = key_cache.shape[1]
    slots_here = key_cache.shape[0]
    page_total = page_table.shape[0]
    prefix_len = page_total * page_size // group_count
    scale = 1.0 / math.sqrt(HD)
    column = lax.axis_index("col")

    rows_n = D // local_width
    cols_n = page_total // slots_here
    row_order = [4, 2, 1, 8] if rows_n == 16 else [1 << i for i in range(rows_n.bit_length() - 1)]
    col_order = [4, 2, 16, 8, 1] if cols_n == 32 else [1 << i for i in range(cols_n.bit_length() - 1)]
    row_parts, weight_all = paired_gathers(
        jnp.concatenate([hidden.T, o_weight], axis=1), "row", rows_n, row_order,
        qkv_weight, "col", cols_n, col_order,
    )
    hidden_t = row_parts[:, :tok_here]
    out_rows = row_parts[:, tok_here:]
    out_weight_t = lax.all_gather(out_rows.T, "col", axis=0, tiled=True)

    projected = jnp.einsum(
        "dt,dcf->tcf", hidden_t, weight_all, preferred_element_type=jnp.float32
    )
    query_raw = projected[:, 0]
    key_raw = projected[:, 1]
    value_raw = projected[:, 2]
    squares = butterfly_sum(
        jnp.stack([jnp.sum(query_raw * query_raw, axis=1), jnp.sum(key_raw * key_raw, axis=1)]),
        "row",
        rows_n,
    )
    query_norm = query_raw * lax.rsqrt(squares[0] / D + EPS)[:, None] * q_gain
    key_norm = key_raw * lax.rsqrt(squares[1] / D + EPS)[:, None] * k_gain
    ends = jnp.cumsum(suffix_lengths)
    starts = ends - suffix_lengths
    my_slot = lax.dynamic_slice_in_dim(token_slot, column * tok_here, tok_here)
    my_group = group_of(my_slot, ends)
    begin = jnp.sum(
        jnp.where(
            my_group[:, None] == jnp.arange(group_count, dtype=jnp.int32)[None, :],
            starts[None, :],
            0,
        ),
        axis=1,
    )
    position = prefix_len + my_slot - begin
    query_rot = rotate(query_norm, position).astype(jnp.bfloat16)
    key_rot = rotate(key_norm, position).astype(jnp.bfloat16)
    value_here = value_raw.astype(jnp.bfloat16)

    all_query = doubling_gather(query_rot, "col", cols_n, col_order)
    their_group = group_of(token_slot, ends)

    page_slots = column * slots_here + jnp.arange(slots_here, dtype=jnp.int32)
    page_index = jnp.sum(
        jnp.where(
            page_table[None, :] == page_slots[:, None],
            jnp.arange(page_total, dtype=jnp.int32)[None, :],
            0,
        ),
        axis=1,
    )
    slot_group = page_index // (page_total // group_count)
    keys = jnp.concatenate([key_cache.reshape(slots_here * page_size, local_width), key_rot])
    values_t = jnp.concatenate(
        [value_cache.reshape(slots_here * page_size, local_width), value_here]
    ).T
    outgoing = local_partials(
        all_query, their_group, token_slot, slot_group, keys, my_group, my_slot, values_t, scale, tok_here
    )
    incoming = lax.all_to_all(outgoing, "col", split_axis=0, concat_axis=0, tiled=True)
    got_acc = incoming[:, :local_width, :].astype(jnp.float32)
    halves = incoming[:, local_width : local_width + 4, :].astype(jnp.float32)
    got_top = halves[:, 0] + halves[:, 1]
    got_sum = halves[:, 2] + halves[:, 3]
    biggest = jnp.max(got_top, axis=0)
    weight_owner = jnp.exp(got_top - biggest[None])
    denominator = jnp.sum(got_sum * weight_owner, axis=0)
    numerator = jnp.sum(got_acc * weight_owner[:, None, :], axis=0)
    attention_t = (numerator / denominator[None, :]).astype(jnp.bfloat16)
    heads_all = doubling_gather(attention_t, "row", rows_n, row_order)
    mixed = jnp.dot(heads_all.T, out_weight_t.T, preferred_element_type=jnp.float32)
    mean_sq = jnp.mean(mixed * mixed, axis=1)
    branch = lax.dynamic_slice_in_dim(mixed, lax.axis_index("row") * local_width, local_width, axis=1)
    result = hidden.astype(jnp.float32) + branch * lax.rsqrt(mean_sq + EPS)[:, None] * norm_gain
    return result


def solution(mesh):
    return jax.shard_map(
        per_device,
        mesh=mesh,
        in_specs=(
            P("col", "row"),
            P("col", None, "row"),
            P("row"),
            P("row"),
            P("col", None, "row"),
            P("col", None, "row"),
            P(),
            P(),
            P(),
            P("row", "col"),
            P("row"),
        ),
        out_specs=P("col", "row"),
        check_vma=False,
    )
```

```python
import math

import jax
import jax.numpy as jnp
import functools

from jax import lax
from jax.experimental import pallas as pl
from jax.experimental.pallas import tpu as pltpu
from jax.sharding import PartitionSpec as P

D = 2048
HD = 128


EPS = 1e-06
THETA = 500000.0
NEG = -1e30


def rotate(states, position):
    half = states.shape[-1] // 2
    freq = THETA ** (-(jnp.arange(half, dtype=jnp.float32) * 2.0 / states.shape[-1]))
    angle = position.astype(jnp.float32)[:, None] * freq[None, :]
    cosine = jnp.cos(angle)
    sine = jnp.sin(angle)
    first = states[..., :half]
    second = states[..., half:]
    return jnp.concatenate(
        [first * cosine - second * sine, second * cosine + first * sine], axis=-1
    )


def group_of(slots, ends):
    return jnp.sum((ends[None, :] <= slots[:, None]).astype(jnp.int32), axis=1)


def butterfly_sum(x, axis, n):
    step = 1
    while step < n:
        x = x + lax.ppermute(x, axis, [(i, i ^ step) for i in range(n)])
        step *= 2
    return x


def halving_scatter(x, axis, n):
    rows = x.shape[0]
    me = lax.axis_index(axis)
    buf = x.reshape(rows, n, x.shape[1] // n)
    step = n // 2
    while step >= 1:
        half = buf.shape[1] // 2
        upper = (me // step) % 2
        keep = lax.dynamic_slice_in_dim(buf, upper * half, half, axis=1)
        send = lax.dynamic_slice_in_dim(buf, (1 - upper) * half, half, axis=1)
        buf = keep + lax.ppermute(send, axis, [(i, i ^ step) for i in range(n)])
        step //= 2
    return buf.reshape(rows, -1)


def exchange_step(buf, axis, n, step):
    other = lax.ppermute(buf, axis, [(i, i ^ step) for i in range(n)])
    upper = (lax.axis_index(axis) // step) % 2
    size = buf.shape[0]
    both = jnp.zeros((2 * size,) + buf.shape[1:], buf.dtype)
    both = lax.dynamic_update_slice_in_dim(both, buf, upper * size, axis=0)
    return lax.dynamic_update_slice_in_dim(both, other, (1 - upper) * size, axis=0)


def member_order(buf, n, order, rest):
    bits = [step.bit_length() - 1 for step in order]
    buf = buf.reshape((2,) * len(order) + rest)
    lead = [len(order) - 1 - s for s in range(len(order))]
    by_bit = sorted(range(len(order)), key=lambda s: -bits[s])
    buf = buf.transpose([lead[s] for s in by_bit] + list(range(len(order), len(order) + len(rest))))
    return buf.reshape((n * rest[0],) + rest[1:])


def doubling_gather(x, axis, n, order):
    buf = x
    for step in order:
        buf = exchange_step(buf, axis, n, step)
    return member_order(buf, n, order, x.shape)


def paired_gathers(first, first_axis, first_n, first_order, second, second_axis, second_n, second_order):
    a, b = first, second
    for k in range(max(len(first_order), len(second_order))):
        if k < len(first_order):
            a = exchange_step(a, first_axis, first_n, first_order[k])
        if k < len(second_order):
            b = exchange_step(b, second_axis, second_n, second_order[k])
        a, b = lax.optimization_barrier((a, b))
    return (
        member_order(a, first_n, first_order, first.shape),
        member_order(b, second_n, second_order, second.shape),
    )


def partial_kernel(q_ref, qg_ref, qs_ref, pg_ref, k_ref, kg_ref, ks_ref, vt_ref, o_ref, *, scale, page):
    scores = lax.dot_general(
        k_ref[...], q_ref[...], (((1,), (1,)), ((), ())), preferred_element_type=jnp.float32
    ) * scale
    q_group = qg_ref[...]
    pages = pg_ref.shape[0]
    parts = [
        jnp.where(q_group == pg_ref[p], scores[p * page : (p + 1) * page], NEG) for p in range(pages)
    ]
    allowed = (kg_ref[...] == q_group) & (ks_ref[...] <= qs_ref[...])
    parts.append(jnp.where(allowed, scores[pages * page :], NEG))
    scores = jnp.concatenate(parts, axis=0)
    top = jnp.max(scores, axis=0, keepdims=True)
    top_hi = top.astype(jnp.bfloat16).astype(jnp.float32)
    top_lo = (top - top_hi).astype(jnp.bfloat16).astype(jnp.float32)
    base = jnp.where(top > 0.5 * NEG, top_hi + top_lo, 0.0)
    weights = jnp.exp(scores - base)
    total = jnp.sum(weights, axis=0, keepdims=True)
    total_hi = total.astype(jnp.bfloat16).astype(jnp.float32)
    total_lo = (total - total_hi).astype(jnp.bfloat16).astype(jnp.float32)
    numer = jnp.dot(vt_ref[...], weights.astype(jnp.bfloat16), preferred_element_type=jnp.float32)
    width = o_ref.shape[2]
    hd = vt_ref.shape[0]
    extra = o_ref.shape[1] - hd
    row = lax.broadcasted_iota(jnp.int32, (extra, top.shape[1]), 0)
    stats = jnp.where(
        row == 0, top_hi, jnp.where(row == 1, top_lo, jnp.where(row == 2, total_hi, jnp.where(row == 3, total_lo, 0.0)))
    )
    for j in range(o_ref.shape[0]):
        cols = slice(j * width, (j + 1) * width)
        o_ref[j, :hd, :] = numer[:, cols].astype(o_ref.dtype)
        o_ref[j, hd:, :] = stats[:, cols].astype(o_ref.dtype)


def local_partials(
    queries, q_group, q_slot, page_group, keys, k_group, k_slot, values_t, scale, owner_rows, block=2048
):
    count, hd = queries.shape
    nk = keys.shape[0]
    tail = k_group.shape[0]
    page = (nk - tail) // page_group.shape[0]
    per = block // owner_rows
    return pl.pallas_call(
        functools.partial(partial_kernel, scale=scale, page=page),
        grid=(count // block,),
        in_specs=[
            pl.BlockSpec((block, hd), lambda i: (i, 0)),
            pl.BlockSpec((1, block), lambda i: (0, i)),
            pl.BlockSpec((1, block), lambda i: (0, i)),
            pl.BlockSpec(memory_space=pltpu.SMEM),
            pl.BlockSpec((nk, hd), lambda i: (0, 0)),
            pl.BlockSpec((tail, 1), lambda i: (0, 0)),
            pl.BlockSpec((tail, 1), lambda i: (0, 0)),
            pl.BlockSpec((hd, nk), lambda i: (0, 0)),
        ],
        out_specs=pl.BlockSpec((per, hd + 4, owner_rows), lambda i: (i, 0, 0)),
        out_shape=jax.ShapeDtypeStruct((count // owner_rows, hd + 4, owner_rows), jnp.bfloat16),
        cost_estimate=pl.CostEstimate(
            flops=4 * count * nk * hd, transcendentals=count * nk,
            bytes_accessed=2 * count * hd + 4 * nk * hd + 2 * count * (hd + 4),
        ),
    )(queries, q_group[None, :], q_slot[None, :], page_group, keys, k_group[:, None], k_slot[:, None], values_t)


def per_device(
    hidden,
    qkv_weight,
    q_gain,
    k_gain,
    key_cache,
    value_cache,
    page_table,
    suffix_lengths,
    token_slot,
    o_weight,
    norm_gain,
):
    tok_here = hidden.shape[0]
    local_width = q_gain.shape[0]
    group_count = suffix_lengths.shape[0]
    page_size = key_cache.shape[1]
    slots_here = key_cache.shape[0]
    page_total = page_table.shape[0]
    prefix_len = page_total * page_size // group_count
    scale = 1.0 / math.sqrt(HD)
    column = lax.axis_index("col")

    rows_n = D // local_width
    cols_n = page_total // slots_here
    row_order = [4, 2, 1, 8] if rows_n == 16 else [1 << i for i in range(rows_n.bit_length() - 1)]
    col_order = [4, 2, 16, 8, 1] if cols_n == 32 else [1 << i for i in range(cols_n.bit_length() - 1)]
    row_parts, weight_all = paired_gathers(
        jnp.concatenate([hidden.T, o_weight], axis=1), "row", rows_n, row_order,
        qkv_weight, "col", cols_n, col_order,
    )
    hidden_t = row_parts[:, :tok_here]
    out_rows = row_parts[:, tok_here:]
    out_weight_t = lax.all_gather(out_rows.T, "col", axis=0, tiled=True)

    projected = jnp.einsum(
        "dt,dcf->tcf", hidden_t, weight_all, preferred_element_type=jnp.float32
    )
    query_raw = projected[:, 0]
    key_raw = projected[:, 1]
    value_raw = projected[:, 2]
    squares = butterfly_sum(
        jnp.stack([jnp.sum(query_raw * query_raw, axis=1), jnp.sum(key_raw * key_raw, axis=1)]),
        "row",
        rows_n,
    )
    query_norm = query_raw * lax.rsqrt(squares[0] / D + EPS)[:, None] * q_gain
    key_norm = key_raw * lax.rsqrt(squares[1] / D + EPS)[:, None] * k_gain
    ends = jnp.cumsum(suffix_lengths)
    starts = ends - suffix_lengths
    my_slot = lax.dynamic_slice_in_dim(token_slot, column * tok_here, tok_here)
    my_group = group_of(my_slot, ends)
    begin = jnp.sum(
        jnp.where(
            my_group[:, None] == jnp.arange(group_count, dtype=jnp.int32)[None, :],
            starts[None, :],
            0,
        ),
        axis=1,
    )
    position = prefix_len + my_slot - begin
    query_rot = rotate(query_norm, position).astype(jnp.bfloat16)
    key_rot = rotate(key_norm, position).astype(jnp.bfloat16)
    value_here = value_raw.astype(jnp.bfloat16)

    all_query = doubling_gather(query_rot, "col", cols_n, col_order)
    their_group = group_of(token_slot, ends)

    page_slots = column * slots_here + jnp.arange(slots_here, dtype=jnp.int32)
    page_index = jnp.sum(
        jnp.where(
            page_table[None, :] == page_slots[:, None],
            jnp.arange(page_total, dtype=jnp.int32)[None, :],
            0,
        ),
        axis=1,
    )
    slot_group = page_index // (page_total // group_count)
    keys = jnp.concatenate([key_cache.reshape(slots_here * page_size, local_width), key_rot])
    values_t = jnp.concatenate(
        [value_cache.reshape(slots_here * page_size, local_width), value_here]
    ).T
    outgoing = local_partials(
        all_query, their_group, token_slot, slot_group, keys, my_group, my_slot, values_t, scale, tok_here
    )
    incoming = lax.all_to_all(outgoing, "col", split_axis=0, concat_axis=0, tiled=True)
    got_acc = incoming[:, :local_width, :].astype(jnp.float32)
    halves = incoming[:, local_width : local_width + 4, :].astype(jnp.float32)
    got_top = halves[:, 0] + halves[:, 1]
    got_sum = halves[:, 2] + halves[:, 3]
    biggest = jnp.max(got_top, axis=0)
    weight_owner = jnp.exp(got_top - biggest[None])
    denominator = jnp.sum(got_sum * weight_owner, axis=0)
    numerator = jnp.sum(got_acc * weight_owner[:, None, :], axis=0)
    attention_t = (numerator / denominator[None, :]).astype(jnp.bfloat16)
    heads_all = doubling_gather(attention_t, "row", rows_n, row_order)
    mixed = jnp.dot(heads_all.T, out_weight_t.T, preferred_element_type=jnp.float32)
    mean_sq = jnp.mean(mixed * mixed, axis=1)
    branch = lax.dynamic_slice_in_dim(mixed, lax.axis_index("row") * local_width, local_width, axis=1)
    result = hidden.astype(jnp.float32) + branch * lax.rsqrt(mean_sq + EPS)[:, None] * norm_gain
    return result


def solution(mesh):
    return jax.shard_map(
        per_device,
        mesh=mesh,
        in_specs=(
            P("col", "row"),
            P("col", None, "row"),
            P("row"),
            P("row"),
            P("col", None, "row"),
            P("col", None, "row"),
            P(),
            P(),
            P(),
            P("row", "col"),
            P("row"),
        ),
        out_specs=P("col", "row"),
        check_vma=False,
    )
```

```python
import math

import jax
import jax.numpy as jnp
import functools

from jax import lax
from jax.experimental import pallas as pl
from jax.experimental.pallas import tpu as pltpu
from jax.sharding import PartitionSpec as P

D = 2048
HD = 128


EPS = 1e-06
THETA = 500000.0
NEG = -1e30


def rotate(states, position):
    half = states.shape[-1] // 2
    freq = THETA ** (-(jnp.arange(half, dtype=jnp.float32) * 2.0 / states.shape[-1]))
    angle = position.astype(jnp.float32)[:, None] * freq[None, :]
    cosine = jnp.cos(angle)
    sine = jnp.sin(angle)
    first = states[..., :half]
    second = states[..., half:]
    return jnp.concatenate(
        [first * cosine - second * sine, second * cosine + first * sine], axis=-1
    )


def group_of(slots, ends):
    return jnp.sum((ends[None, :] <= slots[:, None]).astype(jnp.int32), axis=1)


def butterfly_sum(x, axis, n):
    step = 1
    while step < n:
        x = x + lax.ppermute(x, axis, [(i, i ^ step) for i in range(n)])
        step *= 2
    return x


def halving_scatter(x, axis, n):
    rows = x.shape[0]
    me = lax.axis_index(axis)
    buf = x.reshape(rows, n, x.shape[1] // n)
    step = n // 2
    while step >= 1:
        half = buf.shape[1] // 2
        upper = (me // step) % 2
        keep = lax.dynamic_slice_in_dim(buf, upper * half, half, axis=1)
        send = lax.dynamic_slice_in_dim(buf, (1 - upper) * half, half, axis=1)
        buf = keep + lax.ppermute(send, axis, [(i, i ^ step) for i in range(n)])
        step //= 2
    return buf.reshape(rows, -1)


def exchange_step(buf, axis, n, step):
    other = lax.ppermute(buf, axis, [(i, i ^ step) for i in range(n)])
    upper = (lax.axis_index(axis) // step) % 2
    size = buf.shape[0]
    both = jnp.zeros((2 * size,) + buf.shape[1:], buf.dtype)
    both = lax.dynamic_update_slice_in_dim(both, buf, upper * size, axis=0)
    return lax.dynamic_update_slice_in_dim(both, other, (1 - upper) * size, axis=0)


def member_order(buf, n, order, rest):
    bits = [step.bit_length() - 1 for step in order]
    buf = buf.reshape((2,) * len(order) + rest)
    lead = [len(order) - 1 - s for s in range(len(order))]
    by_bit = sorted(range(len(order)), key=lambda s: -bits[s])
    buf = buf.transpose([lead[s] for s in by_bit] + list(range(len(order), len(order) + len(rest))))
    return buf.reshape((n * rest[0],) + rest[1:])


def doubling_gather(x, axis, n, order):
    buf = x
    for step in order:
        buf = exchange_step(buf, axis, n, step)
    return member_order(buf, n, order, x.shape)


def paired_gathers(first, first_axis, first_n, first_order, second, second_axis, second_n, second_order):
    a, b = first, second
    for k in range(max(len(first_order), len(second_order))):
        if k < len(first_order):
            a = exchange_step(a, first_axis, first_n, first_order[k])
        if k < len(second_order):
            b = exchange_step(b, second_axis, second_n, second_order[k])
        a, b = lax.optimization_barrier((a, b))
    return (
        member_order(a, first_n, first_order, first.shape),
        member_order(b, second_n, second_order, second.shape),
    )


def partial_kernel(q_ref, qg_ref, qs_ref, pg_ref, k_ref, kg_ref, ks_ref, vt_ref, o_ref, *, scale, page):
    scores = lax.dot_general(
        k_ref[...], q_ref[...], (((1,), (1,)), ((), ())), preferred_element_type=jnp.float32
    ) * scale
    q_group = qg_ref[...]
    pages = pg_ref.shape[0]
    parts = [
        jnp.where(q_group == pg_ref[p], scores[p * page : (p + 1) * page], NEG) for p in range(pages)
    ]
    allowed = (kg_ref[...] == q_group) & (ks_ref[...] <= qs_ref[...])
    parts.append(jnp.where(allowed, scores[pages * page :], NEG))
    scores = jnp.concatenate(parts, axis=0)
    top = jnp.max(scores, axis=0, keepdims=True)
    top_hi = top.astype(jnp.bfloat16).astype(jnp.float32)
    top_lo = (top - top_hi).astype(jnp.bfloat16).astype(jnp.float32)
    base = jnp.where(top > 0.5 * NEG, top_hi + top_lo, 0.0)
    weights = jnp.exp(scores - base)
    total = jnp.sum(weights, axis=0, keepdims=True)
    total_hi = total.astype(jnp.bfloat16).astype(jnp.float32)
    total_lo = (total - total_hi).astype(jnp.bfloat16).astype(jnp.float32)
    numer = jnp.dot(vt_ref[...], weights.astype(jnp.bfloat16), preferred_element_type=jnp.float32)
    width = o_ref.shape[2]
    hd = vt_ref.shape[0]
    extra = o_ref.shape[1] - hd
    row = lax.broadcasted_iota(jnp.int32, (extra, top.shape[1]), 0)
    stats = jnp.where(
        row == 0, top_hi, jnp.where(row == 1, top_lo, jnp.where(row == 2, total_hi, jnp.where(row == 3, total_lo, 0.0)))
    )
    for j in range(o_ref.shape[0]):
        cols = slice(j * width, (j + 1) * width)
        o_ref[j, :hd, :] = numer[:, cols].astype(o_ref.dtype)
        o_ref[j, hd:, :] = stats[:, cols].astype(o_ref.dtype)


def local_partials(
    queries, q_group, q_slot, page_group, keys, k_group, k_slot, values_t, scale, owner_rows, block=1024
):
    count, hd = queries.shape
    nk = keys.shape[0]
    tail = k_group.shape[0]
    page = (nk - tail) // page_group.shape[0]
    per = block // owner_rows
    return pl.pallas_call(
        functools.partial(partial_kernel, scale=scale, page=page),
        grid=(count // block,),
        in_specs=[
            pl.BlockSpec((block, hd), lambda i: (i, 0)),
            pl.BlockSpec((1, block), lambda i: (0, i)),
            pl.BlockSpec((1, block), lambda i: (0, i)),
            pl.BlockSpec(memory_space=pltpu.SMEM),
            pl.BlockSpec((nk, hd), lambda i: (0, 0)),
            pl.BlockSpec((tail, 1), lambda i: (0, 0)),
            pl.BlockSpec((tail, 1), lambda i: (0, 0)),
            pl.BlockSpec((hd, nk), lambda i: (0, 0)),
        ],
        out_specs=pl.BlockSpec((per, hd + 4, owner_rows), lambda i: (i, 0, 0)),
        out_shape=jax.ShapeDtypeStruct((count // owner_rows, hd + 4, owner_rows), jnp.bfloat16),
        cost_estimate=pl.CostEstimate(
            flops=4 * count * nk * hd, transcendentals=count * nk,
            bytes_accessed=2 * count * hd + 4 * nk * hd + 2 * count * (hd + 4),
        ),
    )(queries, q_group[None, :], q_slot[None, :], page_group, keys, k_group[:, None], k_slot[:, None], values_t)


def per_device(
    hidden,
    qkv_weight,
    q_gain,
    k_gain,
    key_cache,
    value_cache,
    page_table,
    suffix_lengths,
    token_slot,
    o_weight,
    norm_gain,
):
    tok_here = hidden.shape[0]
    local_width = q_gain.shape[0]
    group_count = suffix_lengths.shape[0]
    page_size = key_cache.shape[1]
    slots_here = key_cache.shape[0]
    page_total = page_table.shape[0]
    prefix_len = page_total * page_size // group_count
    scale = 1.0 / math.sqrt(HD)
    column = lax.axis_index("col")

    rows_n = D // local_width
    cols_n = page_total // slots_here
    row_order = [1, 2, 4, 8] if rows_n == 16 else [1 << i for i in range(rows_n.bit_length() - 1)]
    col_order = [4, 2, 16, 8, 1] if cols_n == 32 else [1 << i for i in range(cols_n.bit_length() - 1)]
    row_parts, weight_all = paired_gathers(
        jnp.concatenate([hidden.T, o_weight], axis=1), "row", rows_n, row_order,
        qkv_weight, "col", cols_n, col_order,
    )
    hidden_t = row_parts[:, :tok_here]
    out_rows = row_parts[:, tok_here:]
    out_weight_t = lax.all_gather(out_rows.T, "col", axis=0, tiled=True)

    projected = jnp.einsum(
        "dt,dcf->tcf", hidden_t, weight_all, preferred_element_type=jnp.float32
    )
    query_raw = projected[:, 0]
    key_raw = projected[:, 1]
    value_raw = projected[:, 2]
    squares = butterfly_sum(
        jnp.stack([jnp.sum(query_raw * query_raw, axis=1), jnp.sum(key_raw * key_raw, axis=1)]),
        "row",
        rows_n,
    )
    query_norm = query_raw * lax.rsqrt(squares[0] / D + EPS)[:, None] * q_gain
    key_norm = key_raw * lax.rsqrt(squares[1] / D + EPS)[:, None] * k_gain
    ends = jnp.cumsum(suffix_lengths)
    starts = ends - suffix_lengths
    my_slot = lax.dynamic_slice_in_dim(token_slot, column * tok_here, tok_here)
    my_group = group_of(my_slot, ends)
    begin = jnp.sum(
        jnp.where(
            my_group[:, None] == jnp.arange(group_count, dtype=jnp.int32)[None, :],
            starts[None, :],
            0,
        ),
        axis=1,
    )
    position = prefix_len + my_slot - begin
    query_rot = rotate(query_norm, position).astype(jnp.bfloat16)
    key_rot = rotate(key_norm, position).astype(jnp.bfloat16)
    value_here = value_raw.astype(jnp.bfloat16)

    all_query = doubling_gather(query_rot, "col", cols_n, col_order)
    their_group = group_of(token_slot, ends)

    page_slots = column * slots_here + jnp.arange(slots_here, dtype=jnp.int32)
    page_index = jnp.sum(
        jnp.where(
            page_table[None, :] == page_slots[:, None],
            jnp.arange(page_total, dtype=jnp.int32)[None, :],
            0,
        ),
        axis=1,
    )
    slot_group = page_index // (page_total // group_count)
    keys = jnp.concatenate([key_cache.reshape(slots_here * page_size, local_width), key_rot])
    values_t = jnp.concatenate(
        [value_cache.reshape(slots_here * page_size, local_width), value_here]
    ).T
    outgoing = local_partials(
        all_query, their_group, token_slot, slot_group, keys, my_group, my_slot, values_t, scale, tok_here
    )
    incoming = lax.all_to_all(outgoing, "col", split_axis=0, concat_axis=0, tiled=True)
    got_acc = incoming[:, :local_width, :].astype(jnp.float32)
    halves = incoming[:, local_width : local_width + 4, :].astype(jnp.float32)
    got_top = halves[:, 0] + halves[:, 1]
    got_sum = halves[:, 2] + halves[:, 3]
    biggest = jnp.max(got_top, axis=0)
    weight_owner = jnp.exp(got_top - biggest[None])
    denominator = jnp.sum(got_sum * weight_owner, axis=0)
    numerator = jnp.sum(got_acc * weight_owner[:, None, :], axis=0)
    attention_t = (numerator / denominator[None, :]).astype(jnp.bfloat16)
    heads_all = doubling_gather(attention_t, "row", rows_n, row_order)
    mixed = jnp.dot(heads_all.T, out_weight_t.T, preferred_element_type=jnp.float32)
    mean_sq = jnp.mean(mixed * mixed, axis=1)
    branch = lax.dynamic_slice_in_dim(mixed, lax.axis_index("row") * local_width, local_width, axis=1)
    result = hidden.astype(jnp.float32) + branch * lax.rsqrt(mean_sq + EPS)[:, None] * norm_gain
    return result


def solution(mesh):
    return jax.shard_map(
        per_device,
        mesh=mesh,
        in_specs=(
            P("col", "row"),
            P("col", None, "row"),
            P("row"),
            P("row"),
            P("col", None, "row"),
            P("col", None, "row"),
            P(),
            P(),
            P(),
            P("row", "col"),
            P("row"),
        ),
        out_specs=P("col", "row"),
        check_vma=False,
    )
```
